128 devices in a mesh: dp: 2 (over core), seq: 16 (over z, x), head: 4 (over y).
Axes of the slice: x: 4, y: 4, z: 4, core: 2. Of those that a mesh axis runs over, the one named last changes fastest.
Arguments:
- queries: bfloat16 [2, 10240, 2048], P('dp', ('seq', 'head')), may hold values from -45 to 45
- key_rows: bfloat16 [2, 10240, 2048], P('dp', ('seq', 'head')), may hold values from -6 to 6
- values: bfloat16 [2, 10240, 2048], P('dp', ('seq', 'head')), may hold values from -6 to 6
- rand_blocks: int32 [160, 16, 4], P('seq', 'head'), may hold values from 0 to 159, as said below
- out_weight: bfloat16 [2048, 2048], P('head'), may hold values from -0.125 to 0.125
- cotangent: bfloat16 [2, 10240, 2048], P('dp', ('seq', 'head')), may hold values from -6 to 6
Outputs:
- layer_out: bfloat16 [2, 10240, 2048], P('dp', ('seq', 'head'))
- grad_queries: bfloat16 [2, 10240, 2048], P('dp', ('seq', 'head'))
- grad_keys: bfloat16 [2, 10240, 2048], P('dp', ('seq', 'head'))
- grad_values: bfloat16 [2, 10240, 2048], P('dp', ('seq', 'head'))
- weight_grad: float32 [2048, 2048], P('head')
The draws below stay inside these ranges and needn't reach their ends.
Inputs may be any that keep to these rules, and one draw needn't show every extreme that they name: `rand_blocks`: key block b lies in range b // 10 of seq. Over the 10 query blocks of one index of seq and the 4 heads of one index of head, at most 15 of the listed random blocks lie in any one range of seq; in every draw, for every index of head, some range of seq receives exactly 15 of them from every index of seq.
All inputs are finite; a program needn't handle non-finite values.
Results may differ from the reference program's by a relative error of at most 0.034.
Values may be sent and summed in bfloat16 or wider, within the bound.
No kernel may reach another device: no remote copies, remote signals or barrier semaphores. Data moves between devices by JAX's collectives and lax.ppermute only.
A program may use at most 192 MiB of HBM per device.

```python
import math
import jax
import jax.numpy as jnp
from jax import lax

NH = 16
HEAD_SIZE = 128
BLOCK_TOKENS = 64
NRAND = 4
D = 2048
HEADS_DEV = 4
QBLK = 10
NBLK = 160
SEQLEN = 10240
DOCS = 2
SLOTS_PER_QUERY = 8
CAP = 15


def draw_queries(key, part):
    normal_field = jax.random.normal(jax.random.fold_in(key, 11), (DOCS, SEQLEN, D), jnp.float32)
    return jnp.clip(normal_field, -6.0, 6.0).astype(jnp.bfloat16)


def draw_key_rows(key, part):
    normal_field = jax.random.normal(jax.random.fold_in(key, 12), (DOCS, SEQLEN, D), jnp.float32)
    return jnp.clip(normal_field, -6.0, 6.0).astype(jnp.bfloat16)


def draw_rand_blocks(key, part):
    range_count = NBLK // QBLK
    group_count = NH // HEADS_DEV
    request_total = HEADS_DEV * QBLK * NRAND
    key_hot = jax.random.fold_in(key, 21)
    key_rest = jax.random.fold_in(key, 22)
    hot_owner = jax.random.randint(key_hot, (group_count,), 0, range_count)
    group_keys = jax.random.split(key_rest, range_count * group_count)

    def draw_group(sub_key, hot_range):
        key_pick = jax.random.fold_in(sub_key, 1)
        key_order = jax.random.fold_in(sub_key, 2)
        key_offset = jax.random.fold_in(sub_key, 3)
        picked = jax.random.permutation(key_pick, (range_count - 1) * CAP)[:request_total - CAP]
        others = (hot_range + 1 + picked // CAP) % range_count
        owners = jnp.concatenate([jnp.full((CAP,), 0, jnp.int32) + hot_range, others.astype(jnp.int32)])
        owners = jax.random.permutation(key_order, owners)
        offsets = jax.random.randint(key_offset, (request_total,), 0, QBLK)
        return (owners * QBLK + offsets).astype(jnp.int32)
    hot_all = jnp.tile(hot_owner, range_count)
    blocks = jax.vmap(draw_group)(group_keys, hot_all)
    blocks = blocks.reshape(range_count, group_count, QBLK, HEADS_DEV, NRAND)
    return jnp.transpose(blocks, (0, 2, 1, 3, 4)).reshape(NBLK, NH, NRAND).astype(jnp.int32)


def shard_levels(stream_key, shape, cuts, smallest, high):
    def one(axis_at, shards_of):
        steps = jax.random.uniform(jax.random.fold_in(jax.random.fold_in(stream_key, 6), axis_at), (shards_of,), jnp.float32, smallest / len(cuts), high / len(cuts))
        return jnp.repeat(jnp.exp(steps), shape[axis_at] // shards_of).reshape((-1,) + (1,) * (len(shape) - axis_at - 1))

    loudness = one(*cuts[0])
    for cut in cuts[1:]:
        loudness = loudness * one(*cut)
    return loudness


def normal_values(stream_key, extent, spread, reach, pieces=(), kind=jnp.bfloat16):
    array = jax.random.normal(stream_key, extent, jnp.float32) * spread
    if len(pieces) > 0:
        array = shard_levels(stream_key, extent, pieces, -0.22, 0.18) * array
    return jnp.clip(array, min=-reach, max=reach).astype(kind)


def setup_inputs(seed: int = 0) -> dict:
    key_of = jax.random.split(jax.random.key(seed), 7)
    queries = draw_queries(jax.random.fold_in(key_of[6], 71), 0)
    key_rows = draw_key_rows(jax.random.fold_in(key_of[6], 71), 0)
    values = normal_values(key_of[2], (DOCS, SEQLEN, D), 1.0, 6.0, ((0, 2), (1, 64)))
    rand_blocks = draw_rand_blocks(jax.random.fold_in(key_of[6], 71), 0)
    out_weight = normal_values(key_of[4], (D, D), D ** -0.5, 0.125, ((0, 4),))
    cotangent = normal_values(key_of[5], (DOCS, SEQLEN, D), 1.0, 6.0, ((0, 2), (1, 64)))
    return {"queries": queries, "key_rows": key_rows, "values": values, "rand_blocks": rand_blocks, "out_weight": out_weight, "cotangent": cotangent}


def rounded_length(values_in):
    return lax.optimization_barrier(values_in.astype(jnp.bfloat16)).astype(jnp.float32)

def head_pass(packed):
    query_head, key_head, value_head, grad_head, random_ids = packed
    number_of_blocks = NBLK
    softmax_scale = 1.0 / math.sqrt(HEAD_SIZE)
    query_block_rows = query_head.reshape(number_of_blocks, BLOCK_TOKENS, HEAD_SIZE).astype(jnp.float32)
    key_block_rows = key_head.reshape(number_of_blocks, BLOCK_TOKENS, HEAD_SIZE)
    value_block_rows = value_head.reshape(number_of_blocks, BLOCK_TOKENS, HEAD_SIZE)
    gradient_blocks = grad_head.reshape(number_of_blocks, BLOCK_TOKENS, HEAD_SIZE).astype(jnp.float32)
    block_ids = jnp.arange(number_of_blocks, dtype=jnp.int32)
    window = jnp.stack([jnp.maximum(block_ids - 1, 0), block_ids, jnp.minimum(block_ids + 1, number_of_blocks - 1), jnp.zeros_like(block_ids)], axis=1)
    block_per_slot = jnp.concatenate([window, random_ids.astype(jnp.int32)], axis=1)
    live_head = jnp.stack([block_ids > 0, block_ids >= 0, block_ids < number_of_blocks - 1, block_ids >= 0], axis=1)
    live_slots = jnp.concatenate([live_head, random_ids >= 0], axis=1)
    live_mask = jnp.repeat(live_slots, BLOCK_TOKENS, axis=1)[:, None, :]
    keys_per_slot = key_block_rows[block_per_slot].reshape(number_of_blocks, SLOTS_PER_QUERY * BLOCK_TOKENS, HEAD_SIZE).astype(jnp.float32)
    values_per_slot = value_block_rows[block_per_slot].reshape(number_of_blocks, SLOTS_PER_QUERY * BLOCK_TOKENS, HEAD_SIZE).astype(jnp.float32)
    scores = jnp.einsum('ibd,ikd->ibk', query_block_rows, keys_per_slot) * softmax_scale
    row_max = lax.optimization_barrier(jnp.max(jnp.where(live_mask, scores, -jnp.inf), axis=-1, keepdims=True))
    weights = jnp.where(live_mask, jnp.exp(scores - row_max), 0.0)
    totals = lax.optimization_barrier(jnp.sum(weights, axis=-1, keepdims=True))
    attn = (jnp.einsum('ibk,ikd->ibd', rounded_length(weights), values_per_slot) / totals).astype(jnp.bfloat16)
    logsum = row_max + jnp.log(totals)
    probability_rows = jnp.where(live_mask, jnp.exp(scores - logsum), 0.0)
    row_delta = lax.optimization_barrier(jnp.sum(gradient_blocks * attn.astype(jnp.float32), axis=-1, keepdims=True))
    dprob = jnp.einsum('ibd,ikd->ibk', gradient_blocks, values_per_slot)
    score_gradient = rounded_length(probability_rows * (dprob - row_delta))
    grad_q = (jnp.einsum('ibk,ikd->ibd', score_gradient, keys_per_slot) * softmax_scale).astype(jnp.bfloat16)
    key_products = (jnp.einsum('nzq,nze->nqe', score_gradient, query_block_rows) * softmax_scale).reshape(number_of_blocks, SLOTS_PER_QUERY, BLOCK_TOKENS, HEAD_SIZE)
    value_products = jnp.einsum('nzq,nze->nqe', rounded_length(probability_rows), gradient_blocks).reshape(number_of_blocks, SLOTS_PER_QUERY, BLOCK_TOKENS, HEAD_SIZE)
    key_products = jnp.concatenate([key_products[:, :4], rounded_length(key_products[:, 4:])], axis=1)
    value_products = jnp.concatenate([value_products[:, :4], rounded_length(value_products[:, 4:])], axis=1)
    grad_k = jnp.zeros((number_of_blocks, BLOCK_TOKENS, HEAD_SIZE), jnp.float32).at[block_per_slot].add(key_products)
    grad_v = jnp.zeros((number_of_blocks, BLOCK_TOKENS, HEAD_SIZE), jnp.float32).at[block_per_slot].add(value_products)
    return (attn.reshape(SEQLEN, HEAD_SIZE), grad_q.reshape(SEQLEN, HEAD_SIZE), grad_k.astype(jnp.bfloat16).reshape(SEQLEN, HEAD_SIZE), grad_v.astype(jnp.bfloat16).reshape(SEQLEN, HEAD_SIZE))

def split_heads(matrix):
    return jnp.transpose(matrix.reshape(SEQLEN, NH, HEAD_SIZE), (1, 0, 2))

def merge_heads(stacked):
    return jnp.transpose(stacked, (1, 0, 2)).reshape(SEQLEN, D)

def reference(queries, key_rows, values, rand_blocks, out_weight, cotangent):
    random_heads = jnp.transpose(rand_blocks, (1, 0, 2))
    weight_grad = jnp.zeros((D, D), jnp.float32)
    outputs, grads_q, grads_k, grads_v = ([], [], [], [])
    for doc_index in range(DOCS):
        grad_attn = jnp.dot(cotangent[doc_index], out_weight.T, preferred_element_type=jnp.float32).astype(jnp.bfloat16)
        attn_h, gq_h, gk_h, gv_h = lax.map(head_pass, (split_heads(queries[doc_index]), split_heads(key_rows[doc_index]), split_heads(values[doc_index]), split_heads(grad_attn), random_heads))
        attn = merge_heads(attn_h)
        outputs.append(jnp.dot(attn, out_weight, preferred_element_type=jnp.float32).astype(jnp.bfloat16))
        weight_grad = weight_grad + jnp.dot(attn.T, cotangent[doc_index], preferred_element_type=jnp.float32)
        grads_q.append(merge_heads(gq_h))
        grads_k.append(merge_heads(gk_h))
        grads_v.append(merge_heads(gv_h))
    weight_grad = weight_grad * (1.0 / math.sqrt(DOCS * SEQLEN))
    return (jnp.stack(outputs), jnp.stack(grads_q), jnp.stack(grads_k), jnp.stack(grads_v), weight_grad)
```

```python
import math

import jax
import jax.numpy as jnp
from jax import lax
from jax.sharding import PartitionSpec as P

HEAD_SIZE = 128
BLOCK_TOKENS = 64


def with_halo(block, sides, width):
    for axis, dim in sides:
        count = lax.axis_size(axis)
        forward = [(i, i + 1) for i in range(count - 1)]
        backward = [(target, source) for source, target in forward]
        low = lax.ppermute(
            lax.slice_in_dim(block, block.shape[dim] - width, None, axis=dim), axis, forward
        )
        high = lax.ppermute(lax.slice_in_dim(block, 0, width, axis=dim), axis, backward)
        block = jnp.concatenate([low, block, high], axis=dim)
    return block


def broadcast_first(block, axis):
    count = lax.axis_size(axis)
    index = lax.axis_index(axis)
    step = 1
    while step < count:
        pairs = [(i, i + step) for i in range(step) if i + step < count]
        got = lax.ppermute(block, axis, pairs)
        block = jnp.where(index >= step, got, block)
        step *= 2
    return block


def reduce_to_first(block, axis):
    count = lax.axis_size(axis)
    step = 1
    while step * 2 < count:
        step *= 2
    while step >= 1:
        pairs = [(i + step, i) for i in range(step) if i + step < count]
        block = block + lax.ppermute(block, axis, pairs)
        step //= 2
    return block


def per_device(queries, key_rows, values, rand_blocks, out_weight, cotangent):
    block_len = BLOCK_TOKENS
    head_dim = HEAD_SIZE
    seq_count = lax.axis_size("seq")
    seq_index = lax.axis_index("seq")
    q_heads, k_heads, v_heads = (
        lax.all_to_all(queries, "head", split_axis=2, concat_axis=1, tiled=True),
        lax.all_to_all(key_rows, "head", split_axis=2, concat_axis=1, tiled=True),
        lax.all_to_all(values, "head", split_axis=2, concat_axis=1, tiled=True),
    )
    q_rows = q_heads[0]
    shard_len = q_rows.shape[0]
    width_cols = q_rows.shape[1]
    head_count = width_cols // head_dim
    block_count = shard_len // block_len
    rand_count = rand_blocks.shape[2]
    key_value = jnp.concatenate([k_heads[0], v_heads[0]], axis=1)
    padded = with_halo(key_value, (("seq", 0),), block_len)
    first_block = broadcast_first(key_value[:block_len], "seq")
    requests = jnp.transpose(rand_blocks, (0, 2, 1)).reshape(-1)
    request_count = requests.shape[0]
    head_of = jnp.arange(request_count, dtype=jnp.int32) % head_count
    capacity = 3 * request_count // (2 * seq_count)
    owners = requests // block_count
    offsets = requests % block_count
    one_hot = (owners[:, None] == jnp.arange(seq_count, dtype=jnp.int32)[None, :]).astype(jnp.int32)
    position = jnp.sum(one_hot * (jnp.cumsum(one_hot, axis=0) - 1), axis=1)
    slot_of = owners * capacity + position
    asked_codes = (
        jnp.full((seq_count * capacity,), -1, jnp.int32)
        .at[slot_of]
        .set(offsets * head_count + head_of)
        .reshape(seq_count, capacity)
    )
    asked_here = lax.all_to_all(asked_codes, "seq", split_axis=0, concat_axis=0, tiled=True)
    slot_total = seq_count * capacity
    pair_count = block_count * head_count
    asked_flat = asked_here.reshape(slot_total)
    serve_hot = (
        asked_flat[:, None] == jnp.arange(pair_count, dtype=jnp.int32)[None, :]
    ).astype(jnp.bfloat16)
    pick_hot = (
        slot_of[:, None] == jnp.arange(slot_total, dtype=jnp.int32)[None, :]
    ).astype(jnp.bfloat16)
    kv_pairs = jnp.transpose(
        key_value.reshape(block_count, block_len, 2, head_count, head_dim), (0, 3, 1, 2, 4)
    ).reshape(pair_count, block_len * 2 * head_dim)
    served = jnp.dot(serve_hot, kv_pairs, preferred_element_type=jnp.float32).astype(jnp.bfloat16)
    served = served.reshape(seq_count, capacity, block_len, 2 * head_dim)
    received = lax.all_to_all(served, "seq", split_axis=0, concat_axis=0, tiled=True)
    far_pairs = jnp.dot(
        pick_hot, received.reshape(slot_total, -1), preferred_element_type=jnp.float32
    ).astype(jnp.bfloat16)
    pair_view = padded.reshape(block_count + 2, block_len, 2, head_count, head_dim)
    window_pairs = jnp.stack(
        [pair_view[:block_count], pair_view[1 : block_count + 1], pair_view[2:]], axis=1
    ).reshape(block_count, 3 * block_len, 2, head_count, head_dim)
    window_keys = window_pairs[:, :, 0]
    window_vals = window_pairs[:, :, 1]
    first_pairs = first_block.reshape(block_len, 2, head_count, head_dim)
    first_keys = first_pairs[:, 0]
    first_vals = first_pairs[:, 1]
    far_view = far_pairs.reshape(block_count, rand_count, head_count, block_len, 2 * head_dim)
    far_keys = far_view[..., :head_dim]
    far_vals = far_view[..., head_dim:]
    global_ids = seq_index * block_count + jnp.arange(block_count, dtype=jnp.int32)
    block_total = seq_count * block_count
    window_live = jnp.stack([global_ids > 0, global_ids >= 0, global_ids < block_total - 1], axis=1)
    window_mask = jnp.repeat(window_live, block_len, axis=1)[None, :, None, :]
    query_blocks = q_rows.reshape(block_count, block_len, head_count, head_dim)
    softmax_scale = 1.0 / math.sqrt(head_dim)
    score_window = (
        jnp.einsum("ibhd,ikhd->hibk", query_blocks, window_keys, preferred_element_type=jnp.float32)
        * softmax_scale
    )
    score_first = (
        jnp.einsum("ibhd,khd->hibk", query_blocks, first_keys, preferred_element_type=jnp.float32)
        * softmax_scale
    )
    score_far = (
        jnp.einsum("ibhd,irhtd->hibrt", query_blocks, far_keys, preferred_element_type=jnp.float32)
        * softmax_scale
    )
    max_window = jnp.max(jnp.where(window_mask, score_window, -jnp.inf), axis=-1, keepdims=True)
    max_first = jnp.max(score_first, axis=-1, keepdims=True)
    max_far = jnp.max(score_far, axis=(-2, -1))[..., None]
    row_max = jnp.maximum(jnp.maximum(max_window, max_first), max_far)
    weight_window = jnp.where(window_mask, jnp.exp(score_window - row_max), 0.0)
    weight_first = jnp.exp(score_first - row_max)
    weight_far = jnp.exp(score_far - row_max[..., None])
    totals = (
        jnp.sum(weight_window, axis=-1, keepdims=True)
        + jnp.sum(weight_first, axis=-1, keepdims=True)
        + jnp.sum(weight_far, axis=(-2, -1))[..., None]
    )
    mixed = jnp.einsum(
        "hibk,ikhd->ibhd",
        weight_window.astype(jnp.bfloat16),
        window_vals,
        preferred_element_type=jnp.float32,
    )
    mixed = mixed + jnp.einsum(
        "hibk,khd->ibhd",
        weight_first.astype(jnp.bfloat16),
        first_vals,
        preferred_element_type=jnp.float32,
    )
    mixed = mixed + jnp.einsum(
        "hibrt,irhtd->ibhd",
        weight_far.astype(jnp.bfloat16),
        far_vals,
        preferred_element_type=jnp.float32,
    )
    totals_rows = jnp.transpose(totals, (1, 2, 0, 3))
    attn = (mixed / totals_rows).astype(jnp.bfloat16)
    logsum = row_max + jnp.log(totals)
    attn_rows = attn.reshape(shard_len, width_cols)
    layer_out = lax.psum_scatter(
        jnp.dot(attn_rows, out_weight, preferred_element_type=jnp.float32),
        "head",
        scatter_dimension=0,
        tiled=True,
    ).astype(jnp.bfloat16)[None]
    piece_flat = lax.all_gather(cotangent, "head", axis=1, tiled=True)[0]
    grad_piece = jnp.dot(piece_flat, out_weight.T, preferred_element_type=jnp.float32).astype(
        jnp.bfloat16
    )
    weight_acc = jnp.dot(attn_rows.T, piece_flat, preferred_element_type=jnp.float32)
    token_total = lax.axis_size("dp") * seq_count * shard_len
    weight_grad = lax.psum(weight_acc, ("dp", "seq")) * (1.0 / math.sqrt(token_total))
    grad_blocks = grad_piece.reshape(block_count, block_len, head_count, head_dim)
    delta_rows = jnp.sum(grad_blocks.astype(jnp.float32) * attn.astype(jnp.float32), axis=-1)
    row_delta = jnp.transpose(delta_rows, (2, 0, 1))[..., None]
    prob_window = jnp.where(window_mask, jnp.exp(score_window - logsum), 0.0)
    prob_first = jnp.exp(score_first - logsum)
    prob_far = jnp.exp(score_far - logsum[..., None])
    dprob_window = jnp.einsum(
        "ibhd,ikhd->hibk", grad_blocks, window_vals, preferred_element_type=jnp.float32
    )
    dprob_first = jnp.einsum(
        "ibhd,khd->hibk", grad_blocks, first_vals, preferred_element_type=jnp.float32
    )
    dprob_far = jnp.einsum(
        "ibhd,irhtd->hibrt", grad_blocks, far_vals, preferred_element_type=jnp.float32
    )
    dscore_window = (prob_window * (dprob_window - row_delta)).astype(jnp.bfloat16)
    dscore_first = (prob_first * (dprob_first - row_delta)).astype(jnp.bfloat16)
    dscore_far = (prob_far * (dprob_far - row_delta[..., None])).astype(jnp.bfloat16)
    grad_q = jnp.einsum(
        "hibk,ikhd->ibhd", dscore_window, window_keys, preferred_element_type=jnp.float32
    )
    grad_q = grad_q + jnp.einsum(
        "hibk,khd->ibhd", dscore_first, first_keys, preferred_element_type=jnp.float32
    )
    grad_q = grad_q + jnp.einsum(
        "hibrt,irhtd->ibhd", dscore_far, far_keys, preferred_element_type=jnp.float32
    )
    grad_q = (grad_q * softmax_scale).astype(jnp.bfloat16)
    key_window = (
        jnp.einsum(
            "hibk,ibhd->ikhd", dscore_window, query_blocks, preferred_element_type=jnp.float32
        )
        * softmax_scale
    )
    value_window = jnp.einsum(
        "hibk,ibhd->ikhd",
        prob_window.astype(jnp.bfloat16),
        grad_blocks,
        preferred_element_type=jnp.float32,
    )
    key_first = (
        jnp.einsum("hibk,ibhd->khd", dscore_first, query_blocks, preferred_element_type=jnp.float32)
        * softmax_scale
    )
    value_first = jnp.einsum(
        "hibk,ibhd->khd",
        prob_first.astype(jnp.bfloat16),
        grad_blocks,
        preferred_element_type=jnp.float32,
    )
    key_far = (
        jnp.einsum(
            "hibrt,ibhd->irhtd", dscore_far, query_blocks, preferred_element_type=jnp.float32
        )
        * softmax_scale
    )
    value_far = jnp.einsum(
        "hibrt,ibhd->irhtd",
        prob_far.astype(jnp.bfloat16),
        grad_blocks,
        preferred_element_type=jnp.float32,
    )
    window_terms = jnp.stack(
        [
            key_window.reshape(block_count, 3, block_len, head_count, head_dim),
            value_window.reshape(block_count, 3, block_len, head_count, head_dim),
        ],
        axis=3,
    )
    grad_pad = jnp.zeros((block_count + 2, block_len, 2, head_count, head_dim), jnp.float32)
    grad_pad = (
        grad_pad.at[:block_count]
        .add(window_terms[:, 0])
        .at[1 : block_count + 1]
        .add(window_terms[:, 1])
        .at[2:]
        .add(window_terms[:, 2])
    )
    global_grad = reduce_to_first(
        jnp.stack([key_first, value_first], axis=1).reshape(block_len, 2 * width_cols), "seq"
    ).reshape(block_len, 2, head_count, head_dim)
    grad_pad = grad_pad.at[1].add(jnp.where(seq_index == 0, global_grad, 0.0))
    rims = jnp.concatenate([grad_pad[0], grad_pad[block_count + 1]], axis=0).reshape(
        2 * block_len, 2 * width_cols
    )
    rim_sums = with_halo(rims.astype(jnp.bfloat16), (("seq", 0),), block_len).astype(rims.dtype)
    core = grad_pad[1 : block_count + 1].reshape(shard_len, 2 * width_cols)
    core = (
        core.at[:block_len]
        .add(rim_sums[:block_len])
        .at[shard_len - block_len :]
        .add(rim_sums[3 * block_len :])
    )
    core = core.reshape(block_count, block_len, 2, head_count, head_dim)
    far_terms = (
        jnp.concatenate([key_far, value_far], axis=-1)
        .reshape(request_count, block_len * 2 * head_dim)
        .astype(jnp.bfloat16)
    )
    outgoing = jnp.dot(pick_hot.T, far_terms, preferred_element_type=jnp.float32).astype(
        jnp.bfloat16
    )
    outgoing = outgoing.reshape(seq_count, capacity, block_len, 2 * head_dim)
    incoming = lax.all_to_all(outgoing, "seq", split_axis=0, concat_axis=0, tiled=True)
    added = jnp.dot(
        serve_hot.T, incoming.reshape(slot_total, -1), preferred_element_type=jnp.float32
    ).reshape(block_count, head_count, block_len, 2, head_dim)
    core = core + jnp.transpose(added, (0, 2, 3, 1, 4))
    grad_k = core[:, :, 0].reshape(shard_len, width_cols).astype(jnp.bfloat16)
    grad_v = core[:, :, 1].reshape(shard_len, width_cols).astype(jnp.bfloat16)
    grad_q_rows = grad_q.reshape(shard_len, width_cols)
    grad_queries, grad_keys, grad_values = (
        lax.all_to_all(grad_q_rows[None], "head", split_axis=1, concat_axis=2, tiled=True),
        lax.all_to_all(grad_k[None], "head", split_axis=1, concat_axis=2, tiled=True),
        lax.all_to_all(grad_v[None], "head", split_axis=1, concat_axis=2, tiled=True),
    )
    return (layer_out, grad_queries, grad_keys, grad_values, weight_grad)


def solution(mesh):
    in_specs = (
        P("dp", ("seq", "head"), None),
        P("dp", ("seq", "head"), None),
        P("dp", ("seq", "head"), None),
        P("seq", "head", None),
        P("head", None),
        P("dp", ("seq", "head"), None),
    )
    out_specs = (
        P("dp", ("seq", "head"), None),
        P("dp", ("seq", "head"), None),
        P("dp", ("seq", "head"), None),
        P("dp", ("seq", "head"), None),
        P("head", None),
    )
    return jax.shard_map(
        per_device, mesh=mesh, in_specs=in_specs, out_specs=out_specs, check_vma=False
    )
```

```python
import math

import jax
import jax.numpy as jnp
from jax import lax
from jax.sharding import PartitionSpec as P

HEAD_SIZE = 128
BLOCK_TOKENS = 64


def with_halo(block, sides, width):
    for axis, dim in sides:
        count = lax.axis_size(axis)
        forward = [(i, i + 1) for i in range(count - 1)]
        backward = [(target, source) for source, target in forward]
        low = lax.ppermute(
            lax.slice_in_dim(block, block.shape[dim] - width, None, axis=dim), axis, forward
        )
        high = lax.ppermute(lax.slice_in_dim(block, 0, width, axis=dim), axis, backward)
        block = jnp.concatenate([low, block, high], axis=dim)
    return block


def broadcast_first(block, axis):
    count = lax.axis_size(axis)
    index = lax.axis_index(axis)
    step = 1
    while step < count:
        pairs = [(i, i + step) for i in range(step) if i + step < count]
        got = lax.ppermute(block, axis, pairs)
        block = jnp.where(index >= step, got, block)
        step *= 2
    return block


def reduce_to_first(block, axis):
    count = lax.axis_size(axis)
    step = 1
    while step * 2 < count:
        step *= 2
    while step >= 1:
        pairs = [(i + step, i) for i in range(step) if i + step < count]
        block = block + lax.ppermute(block, axis, pairs)
        step //= 2
    return block


def per_device(queries, key_rows, values, rand_blocks, out_weight, cotangent):
    block_len = BLOCK_TOKENS
    head_dim = HEAD_SIZE
    seq_count = lax.axis_size("seq")
    seq_index = lax.axis_index("seq")
    group_count = lax.axis_size("head")
    piece_len = queries.shape[1]
    width_cols = queries.shape[2] // group_count
    stacked = jnp.concatenate([queries, key_rows, values], axis=0)
    stacked = jnp.transpose(stacked.reshape(3, piece_len, group_count, width_cols), (2, 0, 1, 3))
    stacked = lax.all_to_all(stacked, "head", split_axis=0, concat_axis=0, tiled=True)
    stacked = jnp.transpose(stacked, (1, 0, 2, 3)).reshape(3, group_count * piece_len, width_cols)
    q_rows = stacked[0]
    shard_len = q_rows.shape[0]
    head_count = width_cols // head_dim
    block_count = shard_len // block_len
    rand_count = rand_blocks.shape[2]
    key_value = jnp.concatenate([stacked[1], stacked[2]], axis=1)
    padded = with_halo(key_value, (("seq", 0),), block_len)
    first_block = broadcast_first(key_value[:block_len], "seq")
    requests = jnp.transpose(rand_blocks, (0, 2, 1)).reshape(-1)
    request_count = requests.shape[0]
    head_of = jnp.arange(request_count, dtype=jnp.int32) % head_count
    capacity = 3 * request_count // (2 * seq_count)
    owners = requests // block_count
    offsets = requests % block_count
    one_hot = (owners[:, None] == jnp.arange(seq_count, dtype=jnp.int32)[None, :]).astype(jnp.int32)
    position = jnp.sum(one_hot * (jnp.cumsum(one_hot, axis=0) - 1), axis=1)
    slot_of = owners * capacity + position
    asked_codes = (
        jnp.full((seq_count * capacity,), -1, jnp.int32)
        .at[slot_of]
        .set(offsets * head_count + head_of)
        .reshape(seq_count, capacity)
    )
    asked_here = lax.all_to_all(asked_codes, "seq", split_axis=0, concat_axis=0, tiled=True)
    slot_total = seq_count * capacity
    pair_count = block_count * head_count
    asked_flat = asked_here.reshape(slot_total)
    serve_hot = (
        asked_flat[:, None] == jnp.arange(pair_count, dtype=jnp.int32)[None, :]
    ).astype(jnp.bfloat16)
    pick_hot = (
        slot_of[:, None] == jnp.arange(slot_total, dtype=jnp.int32)[None, :]
    ).astype(jnp.bfloat16)
    kv_pairs = jnp.transpose(
        key_value.reshape(block_count, block_len, 2, head_count, head_dim), (0, 3, 1, 2, 4)
    ).reshape(pair_count, block_len * 2 * head_dim)
    served = jnp.dot(serve_hot, kv_pairs, preferred_element_type=jnp.float32).astype(jnp.bfloat16)
    served = served.reshape(seq_count, capacity, block_len, 2 * head_dim)
    received = lax.all_to_all(served, "seq", split_axis=0, concat_axis=0, tiled=True)
    far_pairs = jnp.dot(
        pick_hot, received.reshape(slot_total, -1), preferred_element_type=jnp.float32
    ).astype(jnp.bfloat16)
    pair_view = padded.reshape(block_count + 2, block_len, 2, head_count, head_dim)
    window_pairs = jnp.stack(
        [pair_view[:block_count], pair_view[1 : block_count + 1], pair_view[2:]], axis=1
    ).reshape(block_count, 3 * block_len, 2, head_count, head_dim)
    window_keys = window_pairs[:, :, 0]
    window_vals = window_pairs[:, :, 1]
    first_pairs = first_block.reshape(block_len, 2, head_count, head_dim)
    first_keys = first_pairs[:, 0]
    first_vals = first_pairs[:, 1]
    far_view = far_pairs.reshape(block_count, rand_count, head_count, block_len, 2 * head_dim)
    far_keys = far_view[..., :head_dim]
    far_vals = far_view[..., head_dim:]
    global_ids = seq_index * block_count + jnp.arange(block_count, dtype=jnp.int32)
    block_total = seq_count * block_count
    window_live = jnp.stack([global_ids > 0, global_ids >= 0, global_ids < block_total - 1], axis=1)
    window_mask = jnp.repeat(window_live, block_len, axis=1)[None, :, None, :]
    query_blocks = q_rows.reshape(block_count, block_len, head_count, head_dim)
    softmax_scale = 1.0 / math.sqrt(head_dim)
    score_window = (
        jnp.einsum("ibhd,ikhd->hibk", query_blocks, window_keys, preferred_element_type=jnp.float32)
        * softmax_scale
    )
    score_first = (
        jnp.einsum("ibhd,khd->hibk", query_blocks, first_keys, preferred_element_type=jnp.float32)
        * softmax_scale
    )
    score_far = (
        jnp.einsum("ibhd,irhtd->hibrt", query_blocks, far_keys, preferred_element_type=jnp.float32)
        * softmax_scale
    )
    max_window = jnp.max(jnp.where(window_mask, score_window, -jnp.inf), axis=-1, keepdims=True)
    max_first = jnp.max(score_first, axis=-1, keepdims=True)
    max_far = jnp.max(score_far, axis=(-2, -1))[..., None]
    row_max = jnp.maximum(jnp.maximum(max_window, max_first), max_far)
    weight_window = jnp.where(window_mask, jnp.exp(score_window - row_max), 0.0)
    weight_first = jnp.exp(score_first - row_max)
    weight_far = jnp.exp(score_far - row_max[..., None])
    totals = (
        jnp.sum(weight_window, axis=-1, keepdims=True)
        + jnp.sum(weight_first, axis=-1, keepdims=True)
        + jnp.sum(weight_far, axis=(-2, -1))[..., None]
    )
    mixed = jnp.einsum(
        "hibk,ikhd->ibhd",
        weight_window.astype(jnp.bfloat16),
        window_vals,
        preferred_element_type=jnp.float32,
    )
    mixed = mixed + jnp.einsum(
        "hibk,khd->ibhd",
        weight_first.astype(jnp.bfloat16),
        first_vals,
        preferred_element_type=jnp.float32,
    )
    mixed = mixed + jnp.einsum(
        "hibrt,irhtd->ibhd",
        weight_far.astype(jnp.bfloat16),
        far_vals,
        preferred_element_type=jnp.float32,
    )
    totals_rows = jnp.transpose(totals, (1, 2, 0, 3))
    attn = (mixed / totals_rows).astype(jnp.bfloat16)
    logsum = row_max + jnp.log(totals)
    attn_rows = attn.reshape(shard_len, width_cols)
    layer_out = lax.psum_scatter(
        jnp.dot(attn_rows, out_weight, preferred_element_type=jnp.float32),
        "head",
        scatter_dimension=0,
        tiled=True,
    ).astype(jnp.bfloat16)[None]
    piece_flat = lax.all_gather(cotangent, "head", axis=1, tiled=True)[0]
    grad_piece = jnp.dot(piece_flat, out_weight.T, preferred_element_type=jnp.float32).astype(
        jnp.bfloat16
    )
    weight_acc = jnp.dot(attn_rows.T, piece_flat, preferred_element_type=jnp.float32)
    token_total = lax.axis_size("dp") * seq_count * shard_len
    dp_index = lax.axis_index("dp")
    half_rows = width_cols // 2
    mine = lax.dynamic_slice_in_dim(weight_acc, dp_index * half_rows, half_rows, axis=0)
    theirs = lax.dynamic_slice_in_dim(weight_acc, (1 - dp_index) * half_rows, half_rows, axis=0)
    mine = mine + lax.ppermute(theirs, "dp", [(0, 1), (1, 0)])
    mine = lax.psum(mine, "seq") * (1.0 / math.sqrt(token_total))
    other = lax.ppermute(mine, "dp", [(0, 1), (1, 0)])
    weight_grad = jnp.where(
        dp_index == 0,
        jnp.concatenate([mine, other], axis=0),
        jnp.concatenate([other, mine], axis=0),
    )
    grad_blocks = grad_piece.reshape(block_count, block_len, head_count, head_dim)
    delta_rows = jnp.sum(grad_blocks.astype(jnp.float32) * attn.astype(jnp.float32), axis=-1)
    row_delta = jnp.transpose(delta_rows, (2, 0, 1))[..., None]
    prob_window = jnp.where(window_mask, jnp.exp(score_window - logsum), 0.0)
    prob_first = jnp.exp(score_first - logsum)
    prob_far = jnp.exp(score_far - logsum[..., None])
    dprob_window = jnp.einsum(
        "ibhd,ikhd->hibk", grad_blocks, window_vals, preferred_element_type=jnp.float32
    )
    dprob_first = jnp.einsum(
        "ibhd,khd->hibk", grad_blocks, first_vals, preferred_element_type=jnp.float32
    )
    dprob_far = jnp.einsum(
        "ibhd,irhtd->hibrt", grad_blocks, far_vals, preferred_element_type=jnp.float32
    )
    dscore_window = (prob_window * (dprob_window - row_delta)).astype(jnp.bfloat16)
    dscore_first = (prob_first * (dprob_first - row_delta)).astype(jnp.bfloat16)
    dscore_far = (prob_far * (dprob_far - row_delta[..., None])).astype(jnp.bfloat16)
    grad_q = jnp.einsum(
        "hibk,ikhd->ibhd", dscore_window, window_keys, preferred_element_type=jnp.float32
    )
    grad_q = grad_q + jnp.einsum(
        "hibk,khd->ibhd", dscore_first, first_keys, preferred_element_type=jnp.float32
    )
    grad_q = grad_q + jnp.einsum(
        "hibrt,irhtd->ibhd", dscore_far, far_keys, preferred_element_type=jnp.float32
    )
    grad_q = (grad_q * softmax_scale).astype(jnp.bfloat16)
    key_window = (
        jnp.einsum(
            "hibk,ibhd->ikhd", dscore_window, query_blocks, preferred_element_type=jnp.float32
        )
        * softmax_scale
    )
    value_window = jnp.einsum(
        "hibk,ibhd->ikhd",
        prob_window.astype(jnp.bfloat16),
        grad_blocks,
        preferred_element_type=jnp.float32,
    )
    key_first = (
        jnp.einsum("hibk,ibhd->khd", dscore_first, query_blocks, preferred_element_type=jnp.float32)
        * softmax_scale
    )
    value_first = jnp.einsum(
        "hibk,ibhd->khd",
        prob_first.astype(jnp.bfloat16),
        grad_blocks,
        preferred_element_type=jnp.float32,
    )
    key_far = (
        jnp.einsum(
            "hibrt,ibhd->irhtd", dscore_far, query_blocks, preferred_element_type=jnp.float32
        )
        * softmax_scale
    )
    value_far = jnp.einsum(
        "hibrt,ibhd->irhtd",
        prob_far.astype(jnp.bfloat16),
        grad_blocks,
        preferred_element_type=jnp.float32,
    )
    window_terms = jnp.stack(
        [
            key_window.reshape(block_count, 3, block_len, head_count, head_dim),
            value_window.reshape(block_count, 3, block_len, head_count, head_dim),
        ],
        axis=3,
    )
    grad_pad = jnp.zeros((block_count + 2, block_len, 2, head_count, head_dim), jnp.float32)
    grad_pad = (
        grad_pad.at[:block_count]
        .add(window_terms[:, 0])
        .at[1 : block_count + 1]
        .add(window_terms[:, 1])
        .at[2:]
        .add(window_terms[:, 2])
    )
    global_grad = reduce_to_first(
        jnp.stack([key_first, value_first], axis=1).reshape(block_len, 2 * width_cols), "seq"
    ).reshape(block_len, 2, head_count, head_dim)
    grad_pad = grad_pad.at[1].add(jnp.where(seq_index == 0, global_grad, 0.0))
    rims = jnp.concatenate([grad_pad[0], grad_pad[block_count + 1]], axis=0).reshape(
        2 * block_len, 2 * width_cols
    )
    rim_sums = with_halo(rims.astype(jnp.bfloat16), (("seq", 0),), block_len).astype(rims.dtype)
    core = grad_pad[1 : block_count + 1].reshape(shard_len, 2 * width_cols)
    core = (
        core.at[:block_len]
        .add(rim_sums[:block_len])
        .at[shard_len - block_len :]
        .add(rim_sums[3 * block_len :])
    )
    core = core.reshape(block_count, block_len, 2, head_count, head_dim)
    far_terms = (
        jnp.concatenate([key_far, value_far], axis=-1)
        .reshape(request_count, block_len * 2 * head_dim)
        .astype(jnp.bfloat16)
    )
    outgoing = jnp.dot(pick_hot.T, far_terms, preferred_element_type=jnp.float32).astype(
        jnp.bfloat16
    )
    outgoing = outgoing.reshape(seq_count, capacity, block_len, 2 * head_dim)
    incoming = lax.all_to_all(outgoing, "seq", split_axis=0, concat_axis=0, tiled=True)
    added = jnp.dot(
        serve_hot.T, incoming.reshape(slot_total, -1), preferred_element_type=jnp.float32
    ).reshape(block_count, head_count, block_len, 2, head_dim)
    core = core + jnp.transpose(added, (0, 2, 3, 1, 4))
    grad_k = core[:, :, 0].reshape(shard_len, width_cols).astype(jnp.bfloat16)
    grad_v = core[:, :, 1].reshape(shard_len, width_cols).astype(jnp.bfloat16)
    grad_q_rows = grad_q.reshape(shard_len, width_cols)
    back = jnp.stack([grad_q_rows, grad_k, grad_v]).reshape(3, group_count, piece_len, width_cols)
    back = lax.all_to_all(
        jnp.transpose(back, (1, 0, 2, 3)), "head", split_axis=0, concat_axis=0, tiled=True
    )
    back = jnp.transpose(back, (1, 2, 0, 3)).reshape(3, 1, piece_len, group_count * width_cols)
    grad_queries, grad_keys, grad_values = back[0], back[1], back[2]
    return (layer_out, grad_queries, grad_keys, grad_values, weight_grad)


def solution(mesh):
    in_specs = (
        P("dp", ("seq", "head"), None),
        P("dp", ("seq", "head"), None),
        P("dp", ("seq", "head"), None),
        P("seq", "head", None),
        P("head", None),
        P("dp", ("seq", "head"), None),
    )
    out_specs = (
        P("dp", ("seq", "head"), None),
        P("dp", ("seq", "head"), None),
        P("dp", ("seq", "head"), None),
        P("dp", ("seq", "head"), None),
        P("head", None),
    )
    return jax.shard_map(
        per_device, mesh=mesh, in_specs=in_specs, out_specs=out_specs, check_vma=False
    )
```

```python
import math

import jax
import jax.numpy as jnp
from jax import lax
from jax.sharding import PartitionSpec as P

HEAD_SIZE = 128
BLOCK_TOKENS = 64


def with_halo(block, sides, width):
    for axis, dim in sides:
        count = lax.axis_size(axis)
        forward = [(i, i + 1) for i in range(count - 1)]
        backward = [(target, source) for source, target in forward]
        low = lax.ppermute(
            lax.slice_in_dim(block, block.shape[dim] - width, None, axis=dim), axis, forward
        )
        high = lax.ppermute(lax.slice_in_dim(block, 0, width, axis=dim), axis, backward)
        block = jnp.concatenate([low, block, high], axis=dim)
    return block


def broadcast_first(block, axis):
    count = lax.axis_size(axis)
    index = lax.axis_index(axis)
    step = 1
    while step < count:
        pairs = [(i, i + step) for i in range(step) if i + step < count]
        got = lax.ppermute(block, axis, pairs)
        block = jnp.where(index >= step, got, block)
        step *= 2
    return block


def reduce_to_first(block, axis):
    count = lax.axis_size(axis)
    step = 1
    while step * 2 < count:
        step *= 2
    while step >= 1:
        pairs = [(i + step, i) for i in range(step) if i + step < count]
        block = block + lax.ppermute(block, axis, pairs)
        step //= 2
    return block


def per_device(queries, key_rows, values, rand_blocks, out_weight, cotangent):
    block_len = BLOCK_TOKENS
    head_dim = HEAD_SIZE
    seq_count = lax.axis_size("seq")
    seq_index = lax.axis_index("seq")
    group_count = lax.axis_size("head")
    piece_len = queries.shape[1]
    width_cols = queries.shape[2] // group_count
    stacked = jnp.concatenate([queries, key_rows, values], axis=0)
    stacked = jnp.transpose(stacked.reshape(3, piece_len, group_count, width_cols), (2, 0, 1, 3))
    stacked = lax.all_to_all(stacked, "head", split_axis=0, concat_axis=0, tiled=True)
    stacked = jnp.transpose(stacked, (1, 0, 2, 3)).reshape(3, group_count * piece_len, width_cols)
    q_rows = stacked[0]
    shard_len = q_rows.shape[0]
    head_count = width_cols // head_dim
    block_count = shard_len // block_len
    rand_count = rand_blocks.shape[2]
    key_value = jnp.concatenate([stacked[1], stacked[2]], axis=1)
    padded = with_halo(key_value, (("seq", 0),), block_len)
    first_block = broadcast_first(key_value[:block_len], "seq")
    requests = jnp.transpose(rand_blocks, (0, 2, 1)).reshape(-1)
    request_count = requests.shape[0]
    head_of = jnp.arange(request_count, dtype=jnp.int32) % head_count
    capacity = 3 * request_count // (2 * seq_count)
    owners = requests // block_count
    offsets = requests % block_count
    one_hot = (owners[:, None] == jnp.arange(seq_count, dtype=jnp.int32)[None, :]).astype(jnp.int32)
    position = jnp.sum(one_hot * (jnp.cumsum(one_hot, axis=0) - 1), axis=1)
    slot_of = owners * capacity + position
    asked_codes = (
        jnp.full((seq_count * capacity,), -1, jnp.int32)
        .at[slot_of]
        .set(offsets * head_count + head_of)
        .reshape(seq_count, capacity)
    )
    asked_here = lax.all_to_all(asked_codes, "seq", split_axis=0, concat_axis=0, tiled=True)
    slot_total = seq_count * capacity
    pair_count = block_count * head_count
    asked_flat = asked_here.reshape(slot_total)
    serve_hot = (
        asked_flat[:, None] == jnp.arange(pair_count, dtype=jnp.int32)[None, :]
    ).astype(jnp.bfloat16)
    pick_hot = (
        slot_of[:, None] == jnp.arange(slot_total, dtype=jnp.int32)[None, :]
    ).astype(jnp.bfloat16)
    kv_pairs = jnp.transpose(
        key_value.reshape(block_count, block_len, 2, head_count, head_dim), (2, 0, 3, 1, 4)
    ).reshape(2, pair_count, block_len * head_dim)

    def fetch(pairs):
        served = jnp.dot(serve_hot, pairs, preferred_element_type=jnp.float32).astype(jnp.bfloat16)
        served = served.reshape(seq_count, capacity, block_len, head_dim)
        received = lax.all_to_all(served, "seq", split_axis=0, concat_axis=0, tiled=True)
        picked = jnp.dot(
            pick_hot, received.reshape(slot_total, -1), preferred_element_type=jnp.float32
        ).astype(jnp.bfloat16)
        return picked.reshape(block_count, rand_count, head_count, block_len, head_dim)

    far_keys = fetch(kv_pairs[0])
    far_vals = fetch(kv_pairs[1])
    pair_view = padded.reshape(block_count + 2, block_len, 2, head_count, head_dim)
    window_pairs = jnp.stack(
        [pair_view[:block_count], pair_view[1 : block_count + 1], pair_view[2:]], axis=1
    ).reshape(block_count, 3 * block_len, 2, head_count, head_dim)
    window_keys = window_pairs[:, :, 0]
    window_vals = window_pairs[:, :, 1]
    first_pairs = first_block.reshape(block_len, 2, head_count, head_dim)
    first_keys = first_pairs[:, 0]
    first_vals = first_pairs[:, 1]
    global_ids = seq_index * block_count + jnp.arange(block_count, dtype=jnp.int32)
    block_total = seq_count * block_count
    window_live = jnp.stack([global_ids > 0, global_ids >= 0, global_ids < block_total - 1], axis=1)
    window_mask = jnp.repeat(window_live, block_len, axis=1)[None, :, None, :]
    query_blocks = q_rows.reshape(block_count, block_len, head_count, head_dim)
    softmax_scale = 1.0 / math.sqrt(head_dim)
    score_window = (
        jnp.einsum("ibhd,ikhd->hibk", query_blocks, window_keys, preferred_element_type=jnp.float32)
        * softmax_scale
    )
    score_first = (
        jnp.einsum("ibhd,khd->hibk", query_blocks, first_keys, preferred_element_type=jnp.float32)
        * softmax_scale
    )
    score_far = (
        jnp.einsum("ibhd,irhtd->hibrt", query_blocks, far_keys, preferred_element_type=jnp.float32)
        * softmax_scale
    )
    max_window = jnp.max(jnp.where(window_mask, score_window, -jnp.inf), axis=-1, keepdims=True)
    max_first = jnp.max(score_first, axis=-1, keepdims=True)
    max_far = jnp.max(score_far, axis=(-2, -1))[..., None]
    row_max = jnp.maximum(jnp.maximum(max_window, max_first), max_far)
    weight_window = jnp.where(window_mask, jnp.exp(score_window - row_max), 0.0)
    weight_first = jnp.exp(score_first - row_max)
    weight_far = jnp.exp(score_far - row_max[..., None])
    totals = (
        jnp.sum(weight_window, axis=-1, keepdims=True)
        + jnp.sum(weight_first, axis=-1, keepdims=True)
        + jnp.sum(weight_far, axis=(-2, -1))[..., None]
    )
    mixed = jnp.einsum(
        "hibk,ikhd->ibhd",
        weight_window.astype(jnp.bfloat16),
        window_vals,
        preferred_element_type=jnp.float32,
    )
    mixed = mixed + jnp.einsum(
        "hibk,khd->ibhd",
        weight_first.astype(jnp.bfloat16),
        first_vals,
        preferred_element_type=jnp.float32,
    )
    mixed = mixed + jnp.einsum(
        "hibrt,irhtd->ibhd",
        weight_far.astype(jnp.bfloat16),
        far_vals,
        preferred_element_type=jnp.float32,
    )
    totals_rows = jnp.transpose(totals, (1, 2, 0, 3))
    attn = (mixed / totals_rows).astype(jnp.bfloat16)
    logsum = row_max + jnp.log(totals)
    attn_rows = attn.reshape(shard_len, width_cols)
    layer_out = lax.psum_scatter(
        jnp.dot(attn_rows, out_weight, preferred_element_type=jnp.float32),
        "head",
        scatter_dimension=0,
        tiled=True,
    ).astype(jnp.bfloat16)[None]
    piece_flat = lax.all_gather(cotangent, "head", axis=1, tiled=True)[0]
    grad_piece = jnp.dot(piece_flat, out_weight.T, preferred_element_type=jnp.float32).astype(
        jnp.bfloat16
    )
    weight_acc = jnp.dot(attn_rows.T, piece_flat, preferred_element_type=jnp.float32)
    token_total = lax.axis_size("dp") * seq_count * shard_len
    dp_index = lax.axis_index("dp")
    half_rows = width_cols // 2
    mine = lax.dynamic_slice_in_dim(weight_acc, dp_index * half_rows, half_rows, axis=0)
    theirs = lax.dynamic_slice_in_dim(weight_acc, (1 - dp_index) * half_rows, half_rows, axis=0)
    mine = mine + lax.ppermute(theirs, "dp", [(0, 1), (1, 0)])
    mine = lax.psum(mine, "seq") * (1.0 / math.sqrt(token_total))
    other = lax.ppermute(mine, "dp", [(0, 1), (1, 0)])
    weight_grad = jnp.where(
        dp_index == 0,
        jnp.concatenate([mine, other], axis=0),
        jnp.concatenate([other, mine], axis=0),
    )
    grad_blocks = grad_piece.reshape(block_count, block_len, head_count, head_dim)
    delta_rows = jnp.sum(grad_blocks.astype(jnp.float32) * attn.astype(jnp.float32), axis=-1)
    row_delta = jnp.transpose(delta_rows, (2, 0, 1))[..., None]
    prob_window = jnp.where(window_mask, jnp.exp(score_window - logsum), 0.0)
    prob_first = jnp.exp(score_first - logsum)
    prob_far = jnp.exp(score_far - logsum[..., None])
    dprob_window = jnp.einsum(
        "ibhd,ikhd->hibk", grad_blocks, window_vals, preferred_element_type=jnp.float32
    )
    dprob_first = jnp.einsum(
        "ibhd,khd->hibk", grad_blocks, first_vals, preferred_element_type=jnp.float32
    )
    dprob_far = jnp.einsum(
        "ibhd,irhtd->hibrt", grad_blocks, far_vals, preferred_element_type=jnp.float32
    )
    dscore_window = (prob_window * (dprob_window - row_delta)).astype(jnp.bfloat16)
    dscore_first = (prob_first * (dprob_first - row_delta)).astype(jnp.bfloat16)
    dscore_far = (prob_far * (dprob_far - row_delta[..., None])).astype(jnp.bfloat16)
    grad_q = jnp.einsum(
        "hibk,ikhd->ibhd", dscore_window, window_keys, preferred_element_type=jnp.float32
    )
    grad_q = grad_q + jnp.einsum(
        "hibk,khd->ibhd", dscore_first, first_keys, preferred_element_type=jnp.float32
    )
    grad_q = grad_q + jnp.einsum(
        "hibrt,irhtd->ibhd", dscore_far, far_keys, preferred_element_type=jnp.float32
    )
    grad_q = (grad_q * softmax_scale).astype(jnp.bfloat16)
    key_window = (
        jnp.einsum(
            "hibk,ibhd->ikhd", dscore_window, query_blocks, preferred_element_type=jnp.float32
        )
        * softmax_scale
    )
    value_window = jnp.einsum(
        "hibk,ibhd->ikhd",
        prob_window.astype(jnp.bfloat16),
        grad_blocks,
        preferred_element_type=jnp.float32,
    )
    key_first = (
        jnp.einsum("hibk,ibhd->khd", dscore_first, query_blocks, preferred_element_type=jnp.float32)
        * softmax_scale
    )
    value_first = jnp.einsum(
        "hibk,ibhd->khd",
        prob_first.astype(jnp.bfloat16),
        grad_blocks,
        preferred_element_type=jnp.float32,
    )
    key_far = (
        jnp.einsum(
            "hibrt,ibhd->irhtd", dscore_far, query_blocks, preferred_element_type=jnp.float32
        )
        * softmax_scale
    )
    value_far = jnp.einsum(
        "hibrt,ibhd->irhtd",
        prob_far.astype(jnp.bfloat16),
        grad_blocks,
        preferred_element_type=jnp.float32,
    )
    window_terms = jnp.stack(
        [
            key_window.reshape(block_count, 3, block_len, head_count, head_dim),
            value_window.reshape(block_count, 3, block_len, head_count, head_dim),
        ],
        axis=3,
    )
    grad_pad = jnp.zeros((block_count + 2, block_len, 2, head_count, head_dim), jnp.float32)
    grad_pad = (
        grad_pad.at[:block_count]
        .add(window_terms[:, 0])
        .at[1 : block_count + 1]
        .add(window_terms[:, 1])
        .at[2:]
        .add(window_terms[:, 2])
    )
    global_grad = reduce_to_first(
        jnp.stack([key_first, value_first], axis=1).reshape(block_len, 2 * width_cols), "seq"
    ).reshape(block_len, 2, head_count, head_dim)
    grad_pad = grad_pad.at[1].add(jnp.where(seq_index == 0, global_grad, 0.0))
    rims = jnp.concatenate([grad_pad[0], grad_pad[block_count + 1]], axis=0).reshape(
        2 * block_len, 2 * width_cols
    )
    rim_sums = with_halo(rims.astype(jnp.bfloat16), (("seq", 0),), block_len).astype(rims.dtype)
    core = grad_pad[1 : block_count + 1].reshape(shard_len, 2 * width_cols)
    core = (
        core.at[:block_len]
        .add(rim_sums[:block_len])
        .at[shard_len - block_len :]
        .add(rim_sums[3 * block_len :])
    )
    core = core.reshape(block_count, block_len, 2, head_count, head_dim)
    def give_back(terms):
        terms = terms.reshape(request_count, block_len * head_dim).astype(jnp.bfloat16)
        outgoing = jnp.dot(pick_hot.T, terms, preferred_element_type=jnp.float32).astype(
            jnp.bfloat16
        )
        outgoing = outgoing.reshape(seq_count, capacity, block_len, head_dim)
        incoming = lax.all_to_all(outgoing, "seq", split_axis=0, concat_axis=0, tiled=True)
        return jnp.dot(
            serve_hot.T, incoming.reshape(slot_total, -1), preferred_element_type=jnp.float32
        ).reshape(block_count, head_count, block_len, head_dim)

    added_vals = give_back(value_far)
    added_keys = give_back(key_far)
    added = jnp.stack([added_keys, added_vals], axis=3)
    core = core + jnp.transpose(added, (0, 2, 3, 1, 4))
    grad_k = core[:, :, 0].reshape(shard_len, width_cols).astype(jnp.bfloat16)
    grad_v = core[:, :, 1].reshape(shard_len, width_cols).astype(jnp.bfloat16)
    grad_q_rows = grad_q.reshape(shard_len, width_cols)
    back = jnp.stack([grad_q_rows, grad_k, grad_v]).reshape(3, group_count, piece_len, width_cols)
    back = lax.all_to_all(
        jnp.transpose(back, (1, 0, 2, 3)), "head", split_axis=0, concat_axis=0, tiled=True
    )
    back = jnp.transpose(back, (1, 2, 0, 3)).reshape(3, 1, piece_len, group_count * width_cols)
    grad_queries, grad_keys, grad_values = back[0], back[1], back[2]
    return (layer_out, grad_queries, grad_keys, grad_values, weight_grad)


def solution(mesh):
    in_specs = (
        P("dp", ("seq", "head"), None),
        P("dp", ("seq", "head"), None),
        P("dp", ("seq", "head"), None),
        P("seq", "head", None),
        P("head", None),
        P("dp", ("seq", "head"), None),
    )
    out_specs = (
        P("dp", ("seq", "head"), None),
        P("dp", ("seq", "head"), None),
        P("dp", ("seq", "head"), None),
        P("dp", ("seq", "head"), None),
        P("head", None),
    )
    return jax.shard_map(
        per_device, mesh=mesh, in_specs=in_specs, out_specs=out_specs, check_vma=False
    )
```

```python
import math

import jax
import jax.numpy as jnp
from jax import lax
from jax.sharding import PartitionSpec as P

HEAD_SIZE = 128
BLOCK_TOKENS = 64


def with_halo(block, sides, width):
    for axis, dim in sides:
        count = lax.axis_size(axis)
        forward = [(i, i + 1) for i in range(count - 1)]
        backward = [(target, source) for source, target in forward]
        low = lax.ppermute(
            lax.slice_in_dim(block, block.shape[dim] - width, None, axis=dim), axis, forward
        )
        high = lax.ppermute(lax.slice_in_dim(block, 0, width, axis=dim), axis, backward)
        block = jnp.concatenate([low, block, high], axis=dim)
    return block


def broadcast_first(block, axis, radix=4):
    count = lax.axis_size(axis)
    index = lax.axis_index(axis)
    stride = 1
    while stride * radix < count:
        stride *= radix
    while stride >= 1:
        span = stride * radix
        updated = block
        for m in range(1, radix):
            pairs = [(j, j + m * stride) for j in range(0, count, span) if j + m * stride < count]
            if pairs:
                got = lax.ppermute(block, axis, pairs)
                updated = jnp.where(index % span == m * stride, got, updated)
        block = updated
        stride //= radix
    return block


def reduce_to_first(block, axis, radix=4):
    count = lax.axis_size(axis)
    stride = 1
    while stride < count:
        span = stride * radix
        total = block
        for m in range(1, radix):
            pairs = [(j + m * stride, j) for j in range(0, count, span) if j + m * stride < count]
            if pairs:
                total = total + lax.ppermute(block, axis, pairs)
        block = total
        stride *= radix
    return block


def request_slots(rand_blocks, block_count, head_count, seq_count, capacity):
    requests = jnp.transpose(rand_blocks, (0, 2, 1)).reshape(-1)
    head_of = jnp.arange(requests.shape[0], dtype=jnp.int32) % head_count
    owners = requests // block_count
    offsets = requests % block_count
    one_hot = (owners[:, None] == jnp.arange(seq_count, dtype=jnp.int32)[None, :]).astype(jnp.int32)
    position = jnp.sum(one_hot * (jnp.cumsum(one_hot, axis=0) - 1), axis=1)
    return owners, position, offsets * head_count + head_of


def per_device(queries, key_rows, values, rand_blocks, out_weight, cotangent):
    block_len = BLOCK_TOKENS
    head_dim = HEAD_SIZE
    seq_count = lax.axis_size("seq")
    seq_index = lax.axis_index("seq")
    group_count = lax.axis_size("head")
    piece_len = queries.shape[1]
    width_cols = queries.shape[2] // group_count
    stacked = jnp.concatenate([queries, key_rows, values], axis=0)
    stacked = jnp.transpose(stacked.reshape(3, piece_len, group_count, width_cols), (2, 0, 1, 3))
    stacked = lax.all_to_all(stacked, "head", split_axis=0, concat_axis=0, tiled=True)
    stacked = jnp.transpose(stacked, (1, 0, 2, 3)).reshape(3, group_count * piece_len, width_cols)
    q_rows = stacked[0]
    shard_len = q_rows.shape[0]
    head_count = width_cols // head_dim
    block_count = shard_len // block_len
    rand_count = rand_blocks.shape[2]
    key_value = jnp.concatenate([stacked[1], stacked[2]], axis=1)
    padded = with_halo(key_value, (("seq", 0),), block_len)
    first_block = broadcast_first(key_value[:block_len], "seq")
    request_count = rand_blocks.shape[0] * rand_blocks.shape[1] * rand_blocks.shape[2]
    capacity = 3 * request_count // (2 * seq_count)
    owners, position, codes = request_slots(
        rand_blocks, block_count, head_count, seq_count, capacity
    )
    slot_of = owners * capacity + position
    every_block = lax.all_gather(rand_blocks, "seq", axis=0, tiled=False)
    all_owners, all_position, all_codes = jax.vmap(
        lambda r: request_slots(r, block_count, head_count, seq_count, capacity)
    )(every_block)
    match = (all_owners[:, :, None] == seq_index) & (
        all_position[:, :, None] == jnp.arange(capacity, dtype=jnp.int32)[None, None, :]
    )
    asked_here = jnp.sum(jnp.where(match, all_codes[:, :, None] + 1, 0), axis=1) - 1
    slot_total = seq_count * capacity
    pair_count = block_count * head_count
    asked_flat = asked_here.reshape(slot_total)
    serve_hot = (
        asked_flat[:, None] == jnp.arange(pair_count, dtype=jnp.int32)[None, :]
    ).astype(jnp.bfloat16)
    pick_hot = (
        slot_of[:, None] == jnp.arange(slot_total, dtype=jnp.int32)[None, :]
    ).astype(jnp.bfloat16)
    kv_pairs = jnp.transpose(
        key_value.reshape(block_count, block_len, 2, head_count, head_dim), (2, 0, 3, 1, 4)
    ).reshape(2, pair_count, block_len * head_dim)

    def fetch(pairs):
        served = jnp.dot(serve_hot, pairs, preferred_element_type=jnp.float32).astype(jnp.bfloat16)
        served = served.reshape(seq_count, capacity, block_len, head_dim)
        received = lax.all_to_all(served, "seq", split_axis=0, concat_axis=0, tiled=True)
        picked = jnp.dot(
            pick_hot, received.reshape(slot_total, -1), preferred_element_type=jnp.float32
        ).astype(jnp.bfloat16)
        return picked.reshape(block_count, rand_count, head_count, block_len, head_dim)

    far_keys = fetch(kv_pairs[0])
    far_vals = fetch(kv_pairs[1])
    pair_view = padded.reshape(block_count + 2, block_len, 2, head_count, head_dim)
    window_pairs = jnp.stack(
        [pair_view[:block_count], pair_view[1 : block_count + 1], pair_view[2:]], axis=1
    ).reshape(block_count, 3 * block_len, 2, head_count, head_dim)
    window_keys = window_pairs[:, :, 0]
    window_vals = window_pairs[:, :, 1]
    first_pairs = first_block.reshape(block_len, 2, head_count, head_dim)
    first_keys = first_pairs[:, 0]
    first_vals = first_pairs[:, 1]
    global_ids = seq_index * block_count + jnp.arange(block_count, dtype=jnp.int32)
    block_total = seq_count * block_count
    window_live = jnp.stack([global_ids > 0, global_ids >= 0, global_ids < block_total - 1], axis=1)
    window_mask = jnp.repeat(window_live, block_len, axis=1)[None, :, None, :]
    query_blocks = q_rows.reshape(block_count, block_len, head_count, head_dim)
    softmax_scale = 1.0 / math.sqrt(head_dim)
    score_window = (
        jnp.einsum("ibhd,ikhd->hibk", query_blocks, window_keys, preferred_element_type=jnp.float32)
        * softmax_scale
    )
    score_first = (
        jnp.einsum("ibhd,khd->hibk", query_blocks, first_keys, preferred_element_type=jnp.float32)
        * softmax_scale
    )
    score_far = (
        jnp.einsum("ibhd,irhtd->hibrt", query_blocks, far_keys, preferred_element_type=jnp.float32)
        * softmax_scale
    )
    max_window = jnp.max(jnp.where(window_mask, score_window, -jnp.inf), axis=-1, keepdims=True)
    max_first = jnp.max(score_first, axis=-1, keepdims=True)
    max_far = jnp.max(score_far, axis=(-2, -1))[..., None]
    row_max = jnp.maximum(jnp.maximum(max_window, max_first), max_far)
    weight_window = jnp.where(window_mask, jnp.exp(score_window - row_max), 0.0)
    weight_first = jnp.exp(score_first - row_max)
    weight_far = jnp.exp(score_far - row_max[..., None])
    totals = (
        jnp.sum(weight_window, axis=-1, keepdims=True)
        + jnp.sum(weight_first, axis=-1, keepdims=True)
        + jnp.sum(weight_far, axis=(-2, -1))[..., None]
    )
    mixed = jnp.einsum(
        "hibk,ikhd->ibhd",
        weight_window.astype(jnp.bfloat16),
        window_vals,
        preferred_element_type=jnp.float32,
    )
    mixed = mixed + jnp.einsum(
        "hibk,khd->ibhd",
        weight_first.astype(jnp.bfloat16),
        first_vals,
        preferred_element_type=jnp.float32,
    )
    mixed = mixed + jnp.einsum(
        "hibrt,irhtd->ibhd",
        weight_far.astype(jnp.bfloat16),
        far_vals,
        preferred_element_type=jnp.float32,
    )
    totals_rows = jnp.transpose(totals, (1, 2, 0, 3))
    attn = (mixed / totals_rows).astype(jnp.bfloat16)
    logsum = row_max + jnp.log(totals)
    attn_rows = attn.reshape(shard_len, width_cols)
    layer_out = lax.psum_scatter(
        jnp.dot(attn_rows, out_weight, preferred_element_type=jnp.float32),
        "head",
        scatter_dimension=0,
        tiled=True,
    ).astype(jnp.bfloat16)[None]
    piece_flat = lax.all_gather(cotangent, "head", axis=1, tiled=True)[0]
    grad_piece = jnp.dot(piece_flat, out_weight.T, preferred_element_type=jnp.float32).astype(
        jnp.bfloat16
    )
    weight_acc = jnp.dot(attn_rows.T, piece_flat, preferred_element_type=jnp.float32)
    token_total = lax.axis_size("dp") * seq_count * shard_len
    dp_index = lax.axis_index("dp")
    half_rows = width_cols // 2
    mine = lax.dynamic_slice_in_dim(weight_acc, dp_index * half_rows, half_rows, axis=0)
    theirs = lax.dynamic_slice_in_dim(weight_acc, (1 - dp_index) * half_rows, half_rows, axis=0)
    mine = mine + lax.ppermute(theirs, "dp", [(0, 1), (1, 0)])
    mine = lax.psum(mine, "seq") * (1.0 / math.sqrt(token_total))
    other = lax.ppermute(mine, "dp", [(0, 1), (1, 0)])
    weight_grad = jnp.where(
        dp_index == 0,
        jnp.concatenate([mine, other], axis=0),
        jnp.concatenate([other, mine], axis=0),
    )
    grad_blocks = grad_piece.reshape(block_count, block_len, head_count, head_dim)
    delta_rows = jnp.sum(grad_blocks.astype(jnp.float32) * attn.astype(jnp.float32), axis=-1)
    row_delta = jnp.transpose(delta_rows, (2, 0, 1))[..., None]
    prob_window = jnp.where(window_mask, jnp.exp(score_window - logsum), 0.0)
    prob_first = jnp.exp(score_first - logsum)
    prob_far = jnp.exp(score_far - logsum[..., None])
    dprob_window = jnp.einsum(
        "ibhd,ikhd->hibk", grad_blocks, window_vals, preferred_element_type=jnp.float32
    )
    dprob_first = jnp.einsum(
        "ibhd,khd->hibk", grad_blocks, first_vals, preferred_element_type=jnp.float32
    )
    dprob_far = jnp.einsum(
        "ibhd,irhtd->hibrt", grad_blocks, far_vals, preferred_element_type=jnp.float32
    )
    dscore_window = (prob_window * (dprob_window - row_delta)).astype(jnp.bfloat16)
    dscore_first = (prob_first * (dprob_first - row_delta)).astype(jnp.bfloat16)
    dscore_far = (prob_far * (dprob_far - row_delta[..., None])).astype(jnp.bfloat16)
    grad_q = jnp.einsum(
        "hibk,ikhd->ibhd", dscore_window, window_keys, preferred_element_type=jnp.float32
    )
    grad_q = grad_q + jnp.einsum(
        "hibk,khd->ibhd", dscore_first, first_keys, preferred_element_type=jnp.float32
    )
    grad_q = grad_q + jnp.einsum(
        "hibrt,irhtd->ibhd", dscore_far, far_keys, preferred_element_type=jnp.float32
    )
    grad_q = (grad_q * softmax_scale).astype(jnp.bfloat16)
    key_window = (
        jnp.einsum(
            "hibk,ibhd->ikhd", dscore_window, query_blocks, preferred_element_type=jnp.float32
        )
        * softmax_scale
    )
    value_window = jnp.einsum(
        "hibk,ibhd->ikhd",
        prob_window.astype(jnp.bfloat16),
        grad_blocks,
        preferred_element_type=jnp.float32,
    )
    key_first = (
        jnp.einsum("hibk,ibhd->khd", dscore_first, query_blocks, preferred_element_type=jnp.float32)
        * softmax_scale
    )
    value_first = jnp.einsum(
        "hibk,ibhd->khd",
        prob_first.astype(jnp.bfloat16),
        grad_blocks,
        preferred_element_type=jnp.float32,
    )
    key_far = (
        jnp.einsum(
            "hibrt,ibhd->irhtd", dscore_far, query_blocks, preferred_element_type=jnp.float32
        )
        * softmax_scale
    )
    value_far = jnp.einsum(
        "hibrt,ibhd->irhtd",
        prob_far.astype(jnp.bfloat16),
        grad_blocks,
        preferred_element_type=jnp.float32,
    )
    window_terms = jnp.stack(
        [
            key_window.reshape(block_count, 3, block_len, head_count, head_dim),
            value_window.reshape(block_count, 3, block_len, head_count, head_dim),
        ],
        axis=3,
    )
    grad_pad = jnp.zeros((block_count + 2, block_len, 2, head_count, head_dim), jnp.float32)
    grad_pad = (
        grad_pad.at[:block_count]
        .add(window_terms[:, 0])
        .at[1 : block_count + 1]
        .add(window_terms[:, 1])
        .at[2:]
        .add(window_terms[:, 2])
    )
    global_grad = reduce_to_first(
        jnp.stack([key_first, value_first], axis=1).reshape(block_len, 2 * width_cols), "seq"
    ).reshape(block_len, 2, head_count, head_dim)
    grad_pad = grad_pad.at[1].add(jnp.where(seq_index == 0, global_grad, 0.0))
    rims = jnp.concatenate([grad_pad[0], grad_pad[block_count + 1]], axis=0).reshape(
        2 * block_len, 2 * width_cols
    )
    rim_sums = with_halo(rims.astype(jnp.bfloat16), (("seq", 0),), block_len).astype(rims.dtype)
    core = grad_pad[1 : block_count + 1].reshape(shard_len, 2 * width_cols)
    core = (
        core.at[:block_len]
        .add(rim_sums[:block_len])
        .at[shard_len - block_len :]
        .add(rim_sums[3 * block_len :])
    )
    core = core.reshape(block_count, block_len, 2, head_count, head_dim)
    def give_back(terms):
        terms = terms.reshape(request_count, block_len * head_dim).astype(jnp.bfloat16)
        outgoing = jnp.dot(pick_hot.T, terms, preferred_element_type=jnp.float32).astype(
            jnp.bfloat16
        )
        outgoing = outgoing.reshape(seq_count, capacity, block_len, head_dim)
        incoming = lax.all_to_all(outgoing, "seq", split_axis=0, concat_axis=0, tiled=True)
        return jnp.dot(
            serve_hot.T, incoming.reshape(slot_total, -1), preferred_element_type=jnp.float32
        ).reshape(block_count, head_count, block_len, head_dim)

    added_vals = give_back(value_far)
    added_keys = give_back(key_far)
    added = jnp.stack([added_keys, added_vals], axis=3)
    core = core + jnp.transpose(added, (0, 2, 3, 1, 4))
    grad_k = core[:, :, 0].reshape(shard_len, width_cols).astype(jnp.bfloat16)
    grad_v = core[:, :, 1].reshape(shard_len, width_cols).astype(jnp.bfloat16)
    grad_q_rows = grad_q.reshape(shard_len, width_cols)
    def to_owners(rows):
        count = rows.shape[0]
        rows = rows.reshape(count, group_count, piece_len, width_cols)
        rows = lax.all_to_all(
            jnp.transpose(rows, (1, 0, 2, 3)), "head", split_axis=0, concat_axis=0, tiled=True
        )
        return jnp.transpose(rows, (1, 2, 0, 3)).reshape(count, 1, piece_len, group_count * width_cols)

    grad_queries = to_owners(grad_q_rows[None])[0]
    back = to_owners(jnp.stack([grad_k, grad_v]))
    grad_keys, grad_values = back[0], back[1]
    return (layer_out, grad_queries, grad_keys, grad_values, weight_grad)


def solution(mesh):
    in_specs = (
        P("dp", ("seq", "head"), None),
        P("dp", ("seq", "head"), None),
        P("dp", ("seq", "head"), None),
        P("seq", "head", None),
        P("head", None),
        P("dp", ("seq", "head"), None),
    )
    out_specs = (
        P("dp", ("seq", "head"), None),
        P("dp", ("seq", "head"), None),
        P("dp", ("seq", "head"), None),
        P("dp", ("seq", "head"), None),
        P("head", None),
    )
    return jax.shard_map(
        per_device, mesh=mesh, in_specs=in_specs, out_specs=out_specs, check_vma=False
    )
```

```python
import math

import jax
import jax.numpy as jnp
from jax import lax
from jax.sharding import PartitionSpec as P

HEAD_SIZE = 128
BLOCK_TOKENS = 64


def with_halo(block, sides, width):
    for axis, dim in sides:
        count = lax.axis_size(axis)
        forward = [(i, i + 1) for i in range(count - 1)]
        backward = [(target, source) for source, target in forward]
        low = lax.ppermute(
            lax.slice_in_dim(block, block.shape[dim] - width, None, axis=dim), axis, forward
        )
        high = lax.ppermute(lax.slice_in_dim(block, 0, width, axis=dim), axis, backward)
        block = jnp.concatenate([low, block, high], axis=dim)
    return block


def broadcast_first(block, axis, radix=4):
    count = lax.axis_size(axis)
    index = lax.axis_index(axis)
    stride = 1
    while stride * radix < count:
        stride *= radix
    while stride >= 1:
        span = stride * radix
        updated = block
        for m in range(1, radix):
            pairs = [(j, j + m * stride) for j in range(0, count, span) if j + m * stride < count]
            if pairs:
                got = lax.ppermute(block, axis, pairs)
                updated = jnp.where(index % span == m * stride, got, updated)
        block = updated
        stride //= radix
    return block


def reduce_to_first(block, axis, radix=4):
    count = lax.axis_size(axis)
    stride = 1
    while stride < count:
        span = stride * radix
        total = block
        for m in range(1, radix):
            pairs = [(j + m * stride, j) for j in range(0, count, span) if j + m * stride < count]
            if pairs:
                total = total + lax.ppermute(block, axis, pairs)
        block = total
        stride *= radix
    return block


def request_slots(rand_blocks, block_count, head_count, seq_count, capacity):
    requests = jnp.transpose(rand_blocks, (0, 2, 1)).reshape(-1)
    head_of = jnp.arange(requests.shape[0], dtype=jnp.int32) % head_count
    owners = requests // block_count
    offsets = requests % block_count
    one_hot = (owners[:, None] == jnp.arange(seq_count, dtype=jnp.int32)[None, :]).astype(jnp.int32)
    position = jnp.sum(one_hot * (jnp.cumsum(one_hot, axis=0) - 1), axis=1)
    return owners, position, offsets * head_count + head_of


def per_device(queries, key_rows, values, rand_blocks, out_weight, cotangent):
    block_len = BLOCK_TOKENS
    head_dim = HEAD_SIZE
    seq_count = lax.axis_size("seq")
    seq_index = lax.axis_index("seq")
    group_count = lax.axis_size("head")
    piece_len = queries.shape[1]
    width_cols = queries.shape[2] // group_count
    stacked = jnp.concatenate([queries, key_rows, values], axis=0)
    stacked = jnp.transpose(stacked.reshape(3, piece_len, group_count, width_cols), (2, 0, 1, 3))
    stacked = lax.all_to_all(stacked, "head", split_axis=0, concat_axis=0, tiled=True)
    stacked = jnp.transpose(stacked, (1, 0, 2, 3)).reshape(3, group_count * piece_len, width_cols)
    q_rows = stacked[0]
    shard_len = q_rows.shape[0]
    head_count = width_cols // head_dim
    block_count = shard_len // block_len
    rand_count = rand_blocks.shape[2]
    key_value = jnp.concatenate([stacked[1], stacked[2]], axis=1)
    padded = with_halo(key_value, (("seq", 0),), block_len)
    first_block = broadcast_first(key_value[:block_len], "seq")
    request_count = rand_blocks.shape[0] * rand_blocks.shape[1] * rand_blocks.shape[2]
    capacity = 3 * request_count // (2 * seq_count)
    owners, position, codes = request_slots(
        rand_blocks, block_count, head_count, seq_count, capacity
    )
    slot_of = owners * capacity + position
    every_block = lax.all_gather(rand_blocks, "seq", axis=0, tiled=False)
    all_owners, all_position, all_codes = jax.vmap(
        lambda r: request_slots(r, block_count, head_count, seq_count, capacity)
    )(every_block)
    match = (all_owners[:, :, None] == seq_index) & (
        all_position[:, :, None] == jnp.arange(capacity, dtype=jnp.int32)[None, None, :]
    )
    asked_here = jnp.sum(jnp.where(match, all_codes[:, :, None] + 1, 0), axis=1) - 1
    slot_total = seq_count * capacity
    pair_count = block_count * head_count
    asked_flat = asked_here.reshape(slot_total)
    serve_hot = (
        asked_flat[:, None] == jnp.arange(pair_count, dtype=jnp.int32)[None, :]
    ).astype(jnp.bfloat16)
    pick_hot = (
        slot_of[:, None] == jnp.arange(slot_total, dtype=jnp.int32)[None, :]
    ).astype(jnp.bfloat16)
    kv_pairs = jnp.transpose(
        key_value.reshape(block_count, block_len, 2, head_count, head_dim), (2, 0, 3, 1, 4)
    ).reshape(2, pair_count, block_len * head_dim)

    def fetch(pairs):
        served = jnp.dot(serve_hot, pairs, preferred_element_type=jnp.float32).astype(jnp.bfloat16)
        served = served.reshape(seq_count, capacity, block_len, head_dim)
        received = lax.all_to_all(served, "seq", split_axis=0, concat_axis=0, tiled=True)
        picked = jnp.dot(
            pick_hot, received.reshape(slot_total, -1), preferred_element_type=jnp.float32
        ).astype(jnp.bfloat16)
        return picked.reshape(block_count, rand_count, head_count, block_len, head_dim)

    far_keys = fetch(kv_pairs[0])
    far_vals = fetch(kv_pairs[1])
    pair_view = padded.reshape(block_count + 2, block_len, 2, head_count, head_dim)
    window_pairs = jnp.stack(
        [pair_view[:block_count], pair_view[1 : block_count + 1], pair_view[2:]], axis=1
    ).reshape(block_count, 3 * block_len, 2, head_count, head_dim)
    window_keys = window_pairs[:, :, 0]
    window_vals = window_pairs[:, :, 1]
    first_pairs = first_block.reshape(block_len, 2, head_count, head_dim)
    first_keys = first_pairs[:, 0]
    first_vals = first_pairs[:, 1]
    global_ids = seq_index * block_count + jnp.arange(block_count, dtype=jnp.int32)
    block_total = seq_count * block_count
    window_live = jnp.stack([global_ids > 0, global_ids >= 0, global_ids < block_total - 1], axis=1)
    window_mask = jnp.repeat(window_live, block_len, axis=1)[None, :, None, :]
    query_blocks = q_rows.reshape(block_count, block_len, head_count, head_dim)
    softmax_scale = 1.0 / math.sqrt(head_dim)
    score_window = (
        jnp.einsum("ibhd,ikhd->hibk", query_blocks, window_keys, preferred_element_type=jnp.float32)
        * softmax_scale
    )
    score_first = (
        jnp.einsum("ibhd,khd->hibk", query_blocks, first_keys, preferred_element_type=jnp.float32)
        * softmax_scale
    )
    score_far = (
        jnp.einsum("ibhd,irhtd->hibrt", query_blocks, far_keys, preferred_element_type=jnp.float32)
        * softmax_scale
    )
    max_window = jnp.max(jnp.where(window_mask, score_window, -jnp.inf), axis=-1, keepdims=True)
    max_first = jnp.max(score_first, axis=-1, keepdims=True)
    max_far = jnp.max(score_far, axis=(-2, -1))[..., None]
    row_max = jnp.maximum(jnp.maximum(max_window, max_first), max_far)
    weight_window = jnp.where(window_mask, jnp.exp(score_window - row_max), 0.0)
    weight_first = jnp.exp(score_first - row_max)
    weight_far = jnp.exp(score_far - row_max[..., None])
    totals = (
        jnp.sum(weight_window, axis=-1, keepdims=True)
        + jnp.sum(weight_first, axis=-1, keepdims=True)
        + jnp.sum(weight_far, axis=(-2, -1))[..., None]
    )
    mixed = jnp.einsum(
        "hibk,ikhd->ibhd",
        weight_window.astype(jnp.bfloat16),
        window_vals,
        preferred_element_type=jnp.float32,
    )
    mixed = mixed + jnp.einsum(
        "hibk,khd->ibhd",
        weight_first.astype(jnp.bfloat16),
        first_vals,
        preferred_element_type=jnp.float32,
    )
    mixed = mixed + jnp.einsum(
        "hibrt,irhtd->ibhd",
        weight_far.astype(jnp.bfloat16),
        far_vals,
        preferred_element_type=jnp.float32,
    )
    totals_rows = jnp.transpose(totals, (1, 2, 0, 3))
    attn = (mixed / totals_rows).astype(jnp.bfloat16)
    logsum = row_max + jnp.log(totals)
    attn_rows = attn.reshape(shard_len, width_cols)
    head_index = lax.axis_index("head")
    out_parts = jnp.dot(attn_rows, out_weight, preferred_element_type=jnp.float32).reshape(
        group_count, piece_len, -1
    )
    out_sum = lax.dynamic_index_in_dim(out_parts, head_index, axis=0, keepdims=False)
    for shift in range(1, group_count):
        pairs = [(i, (i + shift) % group_count) for i in range(group_count)]
        sent = lax.dynamic_index_in_dim(
            out_parts, (head_index + shift) % group_count, axis=0, keepdims=False
        )
        out_sum = out_sum + lax.ppermute(sent, "head", pairs)
    layer_out = out_sum.astype(jnp.bfloat16)[None]
    piece_flat = lax.all_gather(cotangent, "head", axis=1, tiled=True)[0]
    grad_piece = jnp.dot(piece_flat, out_weight.T, preferred_element_type=jnp.float32).astype(
        jnp.bfloat16
    )
    weight_acc = jnp.dot(attn_rows.T, piece_flat, preferred_element_type=jnp.float32)
    token_total = lax.axis_size("dp") * seq_count * shard_len
    dp_index = lax.axis_index("dp")
    half_rows = width_cols // 2
    mine = lax.dynamic_slice_in_dim(weight_acc, dp_index * half_rows, half_rows, axis=0)
    theirs = lax.dynamic_slice_in_dim(weight_acc, (1 - dp_index) * half_rows, half_rows, axis=0)
    mine = mine + lax.ppermute(theirs, "dp", [(0, 1), (1, 0)])
    mine = lax.psum(mine, "seq") * (1.0 / math.sqrt(token_total))
    other = lax.ppermute(mine, "dp", [(0, 1), (1, 0)])
    weight_grad = jnp.where(
        dp_index == 0,
        jnp.concatenate([mine, other], axis=0),
        jnp.concatenate([other, mine], axis=0),
    )
    grad_blocks = grad_piece.reshape(block_count, block_len, head_count, head_dim)
    delta_rows = jnp.sum(grad_blocks.astype(jnp.float32) * attn.astype(jnp.float32), axis=-1)
    row_delta = jnp.transpose(delta_rows, (2, 0, 1))[..., None]
    prob_window = jnp.where(window_mask, jnp.exp(score_window - logsum), 0.0)
    prob_first = jnp.exp(score_first - logsum)
    prob_far = jnp.exp(score_far - logsum[..., None])
    dprob_window = jnp.einsum(
        "ibhd,ikhd->hibk", grad_blocks, window_vals, preferred_element_type=jnp.float32
    )
    dprob_first = jnp.einsum(
        "ibhd,khd->hibk", grad_blocks, first_vals, preferred_element_type=jnp.float32
    )
    dprob_far = jnp.einsum(
        "ibhd,irhtd->hibrt", grad_blocks, far_vals, preferred_element_type=jnp.float32
    )
    dscore_window = (prob_window * (dprob_window - row_delta)).astype(jnp.bfloat16)
    dscore_first = (prob_first * (dprob_first - row_delta)).astype(jnp.bfloat16)
    dscore_far = (prob_far * (dprob_far - row_delta[..., None])).astype(jnp.bfloat16)
    grad_q = jnp.einsum(
        "hibk,ikhd->ibhd", dscore_window, window_keys, preferred_element_type=jnp.float32
    )
    grad_q = grad_q + jnp.einsum(
        "hibk,khd->ibhd", dscore_first, first_keys, preferred_element_type=jnp.float32
    )
    grad_q = grad_q + jnp.einsum(
        "hibrt,irhtd->ibhd", dscore_far, far_keys, preferred_element_type=jnp.float32
    )
    grad_q = (grad_q * softmax_scale).astype(jnp.bfloat16)
    key_window = (
        jnp.einsum(
            "hibk,ibhd->ikhd", dscore_window, query_blocks, preferred_element_type=jnp.float32
        )
        * softmax_scale
    )
    value_window = jnp.einsum(
        "hibk,ibhd->ikhd",
        prob_window.astype(jnp.bfloat16),
        grad_blocks,
        preferred_element_type=jnp.float32,
    )
    key_first = (
        jnp.einsum("hibk,ibhd->khd", dscore_first, query_blocks, preferred_element_type=jnp.float32)
        * softmax_scale
    )
    value_first = jnp.einsum(
        "hibk,ibhd->khd",
        prob_first.astype(jnp.bfloat16),
        grad_blocks,
        preferred_element_type=jnp.float32,
    )
    key_far = (
        jnp.einsum(
            "hibrt,ibhd->irhtd", dscore_far, query_blocks, preferred_element_type=jnp.float32
        )
        * softmax_scale
    )
    value_far = jnp.einsum(
        "hibrt,ibhd->irhtd",
        prob_far.astype(jnp.bfloat16),
        grad_blocks,
        preferred_element_type=jnp.float32,
    )
    window_terms = jnp.stack(
        [
            key_window.reshape(block_count, 3, block_len, head_count, head_dim),
            value_window.reshape(block_count, 3, block_len, head_count, head_dim),
        ],
        axis=3,
    )
    grad_pad = jnp.zeros((block_count + 2, block_len, 2, head_count, head_dim), jnp.float32)
    grad_pad = (
        grad_pad.at[:block_count]
        .add(window_terms[:, 0])
        .at[1 : block_count + 1]
        .add(window_terms[:, 1])
        .at[2:]
        .add(window_terms[:, 2])
    )
    global_grad = reduce_to_first(
        jnp.stack([key_first, value_first], axis=1).reshape(block_len, 2 * width_cols), "seq"
    ).reshape(block_len, 2, head_count, head_dim)
    grad_pad = grad_pad.at[1].add(jnp.where(seq_index == 0, global_grad, 0.0))
    rims = jnp.concatenate([grad_pad[0], grad_pad[block_count + 1]], axis=0).reshape(
        2 * block_len, 2 * width_cols
    )
    rim_sums = with_halo(rims.astype(jnp.bfloat16), (("seq", 0),), block_len).astype(rims.dtype)
    core = grad_pad[1 : block_count + 1].reshape(shard_len, 2 * width_cols)
    core = (
        core.at[:block_len]
        .add(rim_sums[:block_len])
        .at[shard_len - block_len :]
        .add(rim_sums[3 * block_len :])
    )
    core = core.reshape(block_count, block_len, 2, head_count, head_dim)
    def give_back(terms):
        terms = terms.reshape(request_count, block_len * head_dim).astype(jnp.bfloat16)
        outgoing = jnp.dot(pick_hot.T, terms, preferred_element_type=jnp.float32).astype(
            jnp.bfloat16
        )
        outgoing = outgoing.reshape(seq_count, capacity, block_len, head_dim)
        incoming = lax.all_to_all(outgoing, "seq", split_axis=0, concat_axis=0, tiled=True)
        return jnp.dot(
            serve_hot.T, incoming.reshape(slot_total, -1), preferred_element_type=jnp.float32
        ).reshape(block_count, head_count, block_len, head_dim)

    added_vals = give_back(value_far)
    added_keys = give_back(key_far)
    added = jnp.stack([added_keys, added_vals], axis=3)
    core = core + jnp.transpose(added, (0, 2, 3, 1, 4))
    grad_k = core[:, :, 0].reshape(shard_len, width_cols).astype(jnp.bfloat16)
    grad_v = core[:, :, 1].reshape(shard_len, width_cols).astype(jnp.bfloat16)
    grad_q_rows = grad_q.reshape(shard_len, width_cols)
    def to_owners(rows):
        count = rows.shape[0]
        rows = rows.reshape(count, group_count, piece_len, width_cols)
        rows = lax.all_to_all(
            jnp.transpose(rows, (1, 0, 2, 3)), "head", split_axis=0, concat_axis=0, tiled=True
        )
        return jnp.transpose(rows, (1, 2, 0, 3)).reshape(count, 1, piece_len, group_count * width_cols)

    grad_queries = to_owners(grad_q_rows[None])[0]
    back = to_owners(jnp.stack([grad_k, grad_v]))
    grad_keys, grad_values = back[0], back[1]
    return (layer_out, grad_queries, grad_keys, grad_values, weight_grad)


def solution(mesh):
    in_specs = (
        P("dp", ("seq", "head"), None),
        P("dp", ("seq", "head"), None),
        P("dp", ("seq", "head"), None),
        P("seq", "head", None),
        P("head", None),
        P("dp", ("seq", "head"), None),
    )
    out_specs = (
        P("dp", ("seq", "head"), None),
        P("dp", ("seq", "head"), None),
        P("dp", ("seq", "head"), None),
        P("dp", ("seq", "head"), None),
        P("head", None),
    )
    return jax.shard_map(
        per_device, mesh=mesh, in_specs=in_specs, out_specs=out_specs, check_vma=False
    )
```

```python
import math

import jax
import jax.numpy as jnp
from jax import lax
from jax.sharding import PartitionSpec as P

HEAD_SIZE = 128
BLOCK_TOKENS = 64


def with_halo(block, sides, width):
    for axis, dim in sides:
        count = lax.axis_size(axis)
        forward = [(i, i + 1) for i in range(count - 1)]
        backward = [(target, source) for source, target in forward]
        low = lax.ppermute(
            lax.slice_in_dim(block, block.shape[dim] - width, None, axis=dim), axis, forward
        )
        high = lax.ppermute(lax.slice_in_dim(block, 0, width, axis=dim), axis, backward)
        block = jnp.concatenate([low, block, high], axis=dim)
    return block


def broadcast_first(block, axis, radix=4):
    count = lax.axis_size(axis)
    index = lax.axis_index(axis)
    stride = 1
    while stride * radix < count:
        stride *= radix
    while stride >= 1:
        span = stride * radix
        updated = block
        for m in range(1, radix):
            pairs = [(j, j + m * stride) for j in range(0, count, span) if j + m * stride < count]
            if pairs:
                got = lax.ppermute(block, axis, pairs)
                updated = jnp.where(index % span == m * stride, got, updated)
        block = updated
        stride //= radix
    return block


def reduce_to_first(block, axis, radix=4):
    count = lax.axis_size(axis)
    stride = 1
    while stride < count:
        span = stride * radix
        total = block
        for m in range(1, radix):
            pairs = [(j + m * stride, j) for j in range(0, count, span) if j + m * stride < count]
            if pairs:
                total = total + lax.ppermute(block, axis, pairs)
        block = total
        stride *= radix
    return block


def request_slots(rand_blocks, block_count, head_count, seq_count, capacity):
    requests = jnp.transpose(rand_blocks, (0, 2, 1)).reshape(-1)
    head_of = jnp.arange(requests.shape[0], dtype=jnp.int32) % head_count
    owners = requests // block_count
    offsets = requests % block_count
    one_hot = (owners[:, None] == jnp.arange(seq_count, dtype=jnp.int32)[None, :]).astype(
        jnp.bfloat16
    )
    count = requests.shape[0]
    lower = (
        jnp.arange(count, dtype=jnp.int32)[:, None] >= jnp.arange(count, dtype=jnp.int32)[None, :]
    ).astype(jnp.bfloat16)
    running = jnp.dot(lower, one_hot, preferred_element_type=jnp.float32)
    position = jnp.sum(one_hot.astype(jnp.float32) * (running - 1.0), axis=1).astype(jnp.int32)
    return owners, position, offsets * head_count + head_of


def gather_all(block, axis, radix=4):
    count = lax.axis_size(axis)
    if count != radix * radix:
        return lax.all_gather(block, axis, axis=0, tiled=False)
    index = lax.axis_index(axis)
    for stride in (1, radix):
        place = (index // stride) % radix
        pieces = [block]
        for m in range(1, radix):
            pairs = [
                (i, i - ((i // stride) % radix) * stride + (((i // stride) % radix + m) % radix) * stride)
                for i in range(count)
            ]
            pieces.append(lax.ppermute(block, axis, pairs))
        pieces = jnp.stack(pieces)
        order = (place - jnp.arange(radix, dtype=jnp.int32)) % radix
        block = jnp.take(pieces, order, axis=0)
        if stride > 1:
            block = block.reshape((radix * radix,) + block.shape[2:])
    return block


def per_device(queries, key_rows, values, rand_blocks, out_weight, cotangent):
    block_len = BLOCK_TOKENS
    head_dim = HEAD_SIZE
    seq_count = lax.axis_size("seq")
    seq_index = lax.axis_index("seq")
    group_count = lax.axis_size("head")
    piece_len = queries.shape[1]
    width_cols = queries.shape[2] // group_count
    stacked = jnp.concatenate([queries, key_rows, values], axis=0)
    stacked = jnp.transpose(stacked.reshape(3, piece_len, group_count, width_cols), (2, 0, 1, 3))
    stacked = lax.all_to_all(stacked, "head", split_axis=0, concat_axis=0, tiled=True)
    stacked = jnp.transpose(stacked, (1, 0, 2, 3)).reshape(3, group_count * piece_len, width_cols)
    q_rows = stacked[0]
    shard_len = q_rows.shape[0]
    head_count = width_cols // head_dim
    block_count = shard_len // block_len
    rand_count = rand_blocks.shape[2]
    key_value = jnp.concatenate([stacked[1], stacked[2]], axis=1)
    padded = with_halo(key_value, (("seq", 0),), block_len)
    first_block = broadcast_first(key_value[:block_len], "seq")
    request_count = rand_blocks.shape[0] * rand_blocks.shape[1] * rand_blocks.shape[2]
    capacity = 3 * request_count // (2 * seq_count)
    owners, position, codes = request_slots(
        rand_blocks, block_count, head_count, seq_count, capacity
    )
    slot_of = owners * capacity + position
    every_block = gather_all(rand_blocks, "seq")
    all_owners, all_position, all_codes = jax.vmap(
        lambda r: request_slots(r, block_count, head_count, seq_count, capacity)
    )(every_block)
    match = (all_owners[:, :, None] == seq_index) & (
        all_position[:, :, None] == jnp.arange(capacity, dtype=jnp.int32)[None, None, :]
    )
    asked_here = jnp.sum(jnp.where(match, all_codes[:, :, None] + 1, 0), axis=1) - 1
    slot_total = seq_count * capacity
    pair_count = block_count * head_count
    asked_flat = asked_here.reshape(slot_total)
    serve_hot = (
        asked_flat[:, None] == jnp.arange(pair_count, dtype=jnp.int32)[None, :]
    ).astype(jnp.bfloat16)
    pick_hot = (
        slot_of[:, None] == jnp.arange(slot_total, dtype=jnp.int32)[None, :]
    ).astype(jnp.bfloat16)
    kv_pairs = jnp.transpose(
        key_value.reshape(block_count, block_len, 2, head_count, head_dim), (2, 0, 3, 1, 4)
    ).reshape(2, pair_count, block_len * head_dim)

    def fetch(pairs):
        served = jnp.dot(serve_hot, pairs, preferred_element_type=jnp.float32).astype(jnp.bfloat16)
        served = served.reshape(seq_count, capacity, block_len, head_dim)
        received = lax.all_to_all(served, "seq", split_axis=0, concat_axis=0, tiled=True)
        picked = jnp.dot(
            pick_hot, received.reshape(slot_total, -1), preferred_element_type=jnp.float32
        ).astype(jnp.bfloat16)
        return picked.reshape(block_count, rand_count, head_count, block_len, head_dim)

    far_keys = fetch(kv_pairs[0])
    far_vals = fetch(kv_pairs[1])
    pair_view = padded.reshape(block_count + 2, block_len, 2, head_count, head_dim)
    window_pairs = jnp.stack(
        [pair_view[:block_count], pair_view[1 : block_count + 1], pair_view[2:]], axis=1
    ).reshape(block_count, 3 * block_len, 2, head_count, head_dim)
    window_keys = window_pairs[:, :, 0]
    window_vals = window_pairs[:, :, 1]
    first_pairs = first_block.reshape(block_len, 2, head_count, head_dim)
    first_keys = first_pairs[:, 0]
    first_vals = first_pairs[:, 1]
    global_ids = seq_index * block_count + jnp.arange(block_count, dtype=jnp.int32)
    block_total = seq_count * block_count
    window_live = jnp.stack([global_ids > 0, global_ids >= 0, global_ids < block_total - 1], axis=1)
    window_mask = jnp.repeat(window_live, block_len, axis=1)[None, :, None, :]
    query_blocks = q_rows.reshape(block_count, block_len, head_count, head_dim)
    softmax_scale = 1.0 / math.sqrt(head_dim)
    score_window = (
        jnp.einsum("ibhd,ikhd->hibk", query_blocks, window_keys, preferred_element_type=jnp.float32)
        * softmax_scale
    )
    score_first = (
        jnp.einsum("ibhd,khd->hibk", query_blocks, first_keys, preferred_element_type=jnp.float32)
        * softmax_scale
    )
    score_far = (
        jnp.einsum("ibhd,irhtd->hibrt", query_blocks, far_keys, preferred_element_type=jnp.float32)
        * softmax_scale
    )
    max_window = jnp.max(jnp.where(window_mask, score_window, -jnp.inf), axis=-1, keepdims=True)
    max_first = jnp.max(score_first, axis=-1, keepdims=True)
    max_far = jnp.max(score_far, axis=(-2, -1))[..., None]
    row_max = jnp.maximum(jnp.maximum(max_window, max_first), max_far)
    weight_window = jnp.where(window_mask, jnp.exp(score_window - row_max), 0.0)
    weight_first = jnp.exp(score_first - row_max)
    weight_far = jnp.exp(score_far - row_max[..., None])
    totals = (
        jnp.sum(weight_window, axis=-1, keepdims=True)
        + jnp.sum(weight_first, axis=-1, keepdims=True)
        + jnp.sum(weight_far, axis=(-2, -1))[..., None]
    )
    mixed = jnp.einsum(
        "hibk,ikhd->ibhd",
        weight_window.astype(jnp.bfloat16),
        window_vals,
        preferred_element_type=jnp.float32,
    )
    mixed = mixed + jnp.einsum(
        "hibk,khd->ibhd",
        weight_first.astype(jnp.bfloat16),
        first_vals,
        preferred_element_type=jnp.float32,
    )
    mixed = mixed + jnp.einsum(
        "hibrt,irhtd->ibhd",
        weight_far.astype(jnp.bfloat16),
        far_vals,
        preferred_element_type=jnp.float32,
    )
    totals_rows = jnp.transpose(totals, (1, 2, 0, 3))
    attn = (mixed / totals_rows).astype(jnp.bfloat16)
    logsum = row_max + jnp.log(totals)
    attn_rows = attn.reshape(shard_len, width_cols)
    layer_out = lax.psum_scatter(
        jnp.dot(attn_rows, out_weight, preferred_element_type=jnp.float32),
        "head",
        scatter_dimension=0,
        tiled=True,
    ).astype(jnp.bfloat16)[None]
    piece_flat = lax.all_gather(cotangent, "head", axis=1, tiled=True)[0]
    grad_piece = jnp.dot(piece_flat, out_weight.T, preferred_element_type=jnp.float32).astype(
        jnp.bfloat16
    )
    weight_acc = jnp.dot(attn_rows.T, piece_flat, preferred_element_type=jnp.float32)
    token_total = lax.axis_size("dp") * seq_count * shard_len
    dp_index = lax.axis_index("dp")
    half_rows = width_cols // 2
    mine = lax.dynamic_slice_in_dim(weight_acc, dp_index * half_rows, half_rows, axis=0)
    theirs = lax.dynamic_slice_in_dim(weight_acc, (1 - dp_index) * half_rows, half_rows, axis=0)
    mine = mine + lax.ppermute(theirs, "dp", [(0, 1), (1, 0)])
    mine = lax.psum(mine, "seq") * (1.0 / math.sqrt(token_total))
    other = lax.ppermute(mine, "dp", [(0, 1), (1, 0)])
    weight_grad = jnp.where(
        dp_index == 0,
        jnp.concatenate([mine, other], axis=0),
        jnp.concatenate([other, mine], axis=0),
    )
    grad_blocks = grad_piece.reshape(block_count, block_len, head_count, head_dim)
    delta_rows = jnp.sum(grad_blocks.astype(jnp.float32) * attn.astype(jnp.float32), axis=-1)
    row_delta = jnp.transpose(delta_rows, (2, 0, 1))[..., None]
    prob_window = jnp.where(window_mask, jnp.exp(score_window - logsum), 0.0)
    prob_first = jnp.exp(score_first - logsum)
    prob_far = jnp.exp(score_far - logsum[..., None])
    dprob_window = jnp.einsum(
        "ibhd,ikhd->hibk", grad_blocks, window_vals, preferred_element_type=jnp.float32
    )
    dprob_first = jnp.einsum(
        "ibhd,khd->hibk", grad_blocks, first_vals, preferred_element_type=jnp.float32
    )
    dprob_far = jnp.einsum(
        "ibhd,irhtd->hibrt", grad_blocks, far_vals, preferred_element_type=jnp.float32
    )
    dscore_window = (prob_window * (dprob_window - row_delta)).astype(jnp.bfloat16)
    dscore_first = (prob_first * (dprob_first - row_delta)).astype(jnp.bfloat16)
    dscore_far = (prob_far * (dprob_far - row_delta[..., None])).astype(jnp.bfloat16)
    grad_q = jnp.einsum(
        "hibk,ikhd->ibhd", dscore_window, window_keys, preferred_element_type=jnp.float32
    )
    grad_q = grad_q + jnp.einsum(
        "hibk,khd->ibhd", dscore_first, first_keys, preferred_element_type=jnp.float32
    )
    grad_q = grad_q + jnp.einsum(
        "hibrt,irhtd->ibhd", dscore_far, far_keys, preferred_element_type=jnp.float32
    )
    grad_q = (grad_q * softmax_scale).astype(jnp.bfloat16)
    key_window = (
        jnp.einsum(
            "hibk,ibhd->ikhd", dscore_window, query_blocks, preferred_element_type=jnp.float32
        )
        * softmax_scale
    )
    value_window = jnp.einsum(
        "hibk,ibhd->ikhd",
        prob_window.astype(jnp.bfloat16),
        grad_blocks,
        preferred_element_type=jnp.float32,
    )
    key_first = (
        jnp.einsum("hibk,ibhd->khd", dscore_first, query_blocks, preferred_element_type=jnp.float32)
        * softmax_scale
    )
    value_first = jnp.einsum(
        "hibk,ibhd->khd",
        prob_first.astype(jnp.bfloat16),
        grad_blocks,
        preferred_element_type=jnp.float32,
    )
    key_far = (
        jnp.einsum(
            "hibrt,ibhd->irhtd", dscore_far, query_blocks, preferred_element_type=jnp.float32
        )
        * softmax_scale
    )
    value_far = jnp.einsum(
        "hibrt,ibhd->irhtd",
        prob_far.astype(jnp.bfloat16),
        grad_blocks,
        preferred_element_type=jnp.float32,
    )
    window_terms = jnp.stack(
        [
            key_window.reshape(block_count, 3, block_len, head_count, head_dim),
            value_window.reshape(block_count, 3, block_len, head_count, head_dim),
        ],
        axis=3,
    )
    grad_pad = jnp.zeros((block_count + 2, block_len, 2, head_count, head_dim), jnp.float32)
    grad_pad = (
        grad_pad.at[:block_count]
        .add(window_terms[:, 0])
        .at[1 : block_count + 1]
        .add(window_terms[:, 1])
        .at[2:]
        .add(window_terms[:, 2])
    )
    global_grad = reduce_to_first(
        jnp.stack([key_first, value_first], axis=1).reshape(block_len, 2 * width_cols), "seq"
    ).reshape(block_len, 2, head_count, head_dim)
    grad_pad = grad_pad.at[1].add(jnp.where(seq_index == 0, global_grad, 0.0))
    rims = jnp.concatenate([grad_pad[0], grad_pad[block_count + 1]], axis=0).reshape(
        2 * block_len, 2 * width_cols
    )
    rim_sums = with_halo(rims.astype(jnp.bfloat16), (("seq", 0),), block_len).astype(rims.dtype)
    core = grad_pad[1 : block_count + 1].reshape(shard_len, 2 * width_cols)
    core = (
        core.at[:block_len]
        .add(rim_sums[:block_len])
        .at[shard_len - block_len :]
        .add(rim_sums[3 * block_len :])
    )
    core = core.reshape(block_count, block_len, 2, head_count, head_dim)
    def give_back(terms):
        terms = terms.reshape(request_count, block_len * head_dim).astype(jnp.bfloat16)
        outgoing = jnp.dot(pick_hot.T, terms, preferred_element_type=jnp.float32).astype(
            jnp.bfloat16
        )
        outgoing = outgoing.reshape(seq_count, capacity, block_len, head_dim)
        incoming = lax.all_to_all(outgoing, "seq", split_axis=0, concat_axis=0, tiled=True)
        return jnp.dot(
            serve_hot.T, incoming.reshape(slot_total, -1), preferred_element_type=jnp.float32
        ).reshape(block_count, head_count, block_len, head_dim)

    added_vals = give_back(value_far)
    added_keys = give_back(key_far)
    added = jnp.stack([added_keys, added_vals], axis=3)
    core = core + jnp.transpose(added, (0, 2, 3, 1, 4))
    grad_k = core[:, :, 0].reshape(shard_len, width_cols).astype(jnp.bfloat16)
    grad_v = core[:, :, 1].reshape(shard_len, width_cols).astype(jnp.bfloat16)
    grad_q_rows = grad_q.reshape(shard_len, width_cols)
    def to_owners(rows):
        count = rows.shape[0]
        rows = rows.reshape(count, group_count, piece_len, width_cols)
        rows = lax.all_to_all(
            jnp.transpose(rows, (1, 0, 2, 3)), "head", split_axis=0, concat_axis=0, tiled=True
        )
        return jnp.transpose(rows, (1, 2, 0, 3)).reshape(count, 1, piece_len, group_count * width_cols)

    grad_queries = to_owners(grad_q_rows[None])[0]
    back = to_owners(jnp.stack([grad_k, grad_v]))
    grad_keys, grad_values = back[0], back[1]
    return (layer_out, grad_queries, grad_keys, grad_values, weight_grad)


def solution(mesh):
    in_specs = (
        P("dp", ("seq", "head"), None),
        P("dp", ("seq", "head"), None),
        P("dp", ("seq", "head"), None),
        P("seq", "head", None),
        P("head", None),
        P("dp", ("seq", "head"), None),
    )
    out_specs = (
        P("dp", ("seq", "head"), None),
        P("dp", ("seq", "head"), None),
        P("dp", ("seq", "head"), None),
        P("dp", ("seq", "head"), None),
        P("head", None),
    )
    return jax.shard_map(
        per_device, mesh=mesh, in_specs=in_specs, out_specs=out_specs, check_vma=False
    )
```

```python
import math

import jax
import jax.numpy as jnp
from jax import lax
from jax.sharding import PartitionSpec as P

HEAD_SIZE = 128
BLOCK_TOKENS = 64


def with_halo(block, sides, width):
    for axis, dim in sides:
        count = lax.axis_size(axis)
        forward = [(i, i + 1) for i in range(count - 1)]
        backward = [(target, source) for source, target in forward]
        low = lax.ppermute(
            lax.slice_in_dim(block, block.shape[dim] - width, None, axis=dim), axis, forward
        )
        high = lax.ppermute(lax.slice_in_dim(block, 0, width, axis=dim), axis, backward)
        block = jnp.concatenate([low, block, high], axis=dim)
    return block


def broadcast_first(block, axis, radix=4):
    count = lax.axis_size(axis)
    index = lax.axis_index(axis)
    stride = 1
    while stride * radix < count:
        stride *= radix
    while stride >= 1:
        span = stride * radix
        updated = block
        for m in range(1, radix):
            pairs = [(j, j + m * stride) for j in range(0, count, span) if j + m * stride < count]
            if pairs:
                got = lax.ppermute(block, axis, pairs)
                updated = jnp.where(index % span == m * stride, got, updated)
        block = updated
        stride //= radix
    return block


def reduce_to_first(block, axis, radix=4):
    count = lax.axis_size(axis)
    stride = 1
    while stride < count:
        span = stride * radix
        total = block
        for m in range(1, radix):
            pairs = [(j + m * stride, j) for j in range(0, count, span) if j + m * stride < count]
            if pairs:
                total = total + lax.ppermute(block, axis, pairs)
        block = total
        stride *= radix
    return block


def request_slots(rand_blocks, block_count, head_count, seq_count, capacity):
    requests = jnp.transpose(rand_blocks, (0, 2, 1)).reshape(-1)
    head_of = jnp.arange(requests.shape[0], dtype=jnp.int32) % head_count
    owners = requests // block_count
    offsets = requests % block_count
    one_hot = (owners[:, None] == jnp.arange(seq_count, dtype=jnp.int32)[None, :]).astype(
        jnp.bfloat16
    )
    count = requests.shape[0]
    lower = (
        jnp.arange(count, dtype=jnp.int32)[:, None] >= jnp.arange(count, dtype=jnp.int32)[None, :]
    ).astype(jnp.bfloat16)
    running = jnp.dot(lower, one_hot, preferred_element_type=jnp.float32)
    position = jnp.sum(one_hot.astype(jnp.float32) * (running - 1.0), axis=1).astype(jnp.int32)
    return owners, position, offsets * head_count + head_of


def gather_all(block, axis, radix=4):
    count = lax.axis_size(axis)
    if count != radix * radix:
        return lax.all_gather(block, axis, axis=0, tiled=False)
    index = lax.axis_index(axis)
    for stride in (1, radix):
        place = (index // stride) % radix
        pieces = [block]
        for m in range(1, radix):
            pairs = [
                (i, i - ((i // stride) % radix) * stride + (((i // stride) % radix + m) % radix) * stride)
                for i in range(count)
            ]
            pieces.append(lax.ppermute(block, axis, pairs))
        pieces = jnp.stack(pieces)
        order = (place - jnp.arange(radix, dtype=jnp.int32)) % radix
        block = jnp.take(pieces, order, axis=0)
        if stride > 1:
            block = block.reshape((radix * radix,) + block.shape[2:])
    return block


def per_device(queries, key_rows, values, rand_blocks, out_weight, cotangent):
    block_len = BLOCK_TOKENS
    head_dim = HEAD_SIZE
    seq_count = lax.axis_size("seq")
    seq_index = lax.axis_index("seq")
    group_count = lax.axis_size("head")
    piece_len = queries.shape[1]
    width_cols = queries.shape[2] // group_count
    stacked = jnp.concatenate([queries, key_rows, values], axis=0)
    stacked = jnp.transpose(stacked.reshape(3, piece_len, group_count, width_cols), (2, 0, 1, 3))
    stacked = lax.all_to_all(stacked, "head", split_axis=0, concat_axis=0, tiled=True)
    stacked = jnp.transpose(stacked, (1, 0, 2, 3)).reshape(3, group_count * piece_len, width_cols)
    q_rows = stacked[0]
    shard_len = q_rows.shape[0]
    head_count = width_cols // head_dim
    block_count = shard_len // block_len
    rand_count = rand_blocks.shape[2]
    key_value = jnp.concatenate([stacked[1], stacked[2]], axis=1)
    padded = with_halo(key_value, (("seq", 0),), block_len)
    first_block = broadcast_first(key_value[:block_len], "seq")
    request_count = rand_blocks.shape[0] * rand_blocks.shape[1] * rand_blocks.shape[2]
    capacity = 3 * request_count // (2 * seq_count)
    owners, position, codes = request_slots(
        rand_blocks, block_count, head_count, seq_count, capacity
    )
    slot_of = owners * capacity + position
    every_block = gather_all(rand_blocks, "seq")
    all_owners, all_position, all_codes = jax.vmap(
        lambda r: request_slots(r, block_count, head_count, seq_count, capacity)
    )(every_block)
    match = (all_owners[:, :, None] == seq_index) & (
        all_position[:, :, None] == jnp.arange(capacity, dtype=jnp.int32)[None, None, :]
    )
    asked_here = jnp.sum(jnp.where(match, all_codes[:, :, None] + 1, 0), axis=1) - 1
    slot_total = seq_count * capacity
    pair_count = block_count * head_count
    asked_flat = asked_here.reshape(slot_total)
    serve_hot = (
        asked_flat[:, None] == jnp.arange(pair_count, dtype=jnp.int32)[None, :]
    ).astype(jnp.bfloat16)
    pick_hot = (
        slot_of[:, None] == jnp.arange(slot_total, dtype=jnp.int32)[None, :]
    ).astype(jnp.bfloat16)
    kv_pairs = jnp.transpose(
        key_value.reshape(block_count, block_len, 2, head_count, head_dim), (2, 0, 3, 1, 4)
    ).reshape(2, pair_count, block_len * head_dim)

    def fetch(pairs):
        served = jnp.dot(serve_hot, pairs, preferred_element_type=jnp.float32).astype(jnp.bfloat16)
        served = served.reshape(seq_count, capacity, block_len, head_dim)
        received = lax.all_to_all(served, "seq", split_axis=0, concat_axis=0, tiled=True)
        picked = jnp.dot(
            pick_hot, received.reshape(slot_total, -1), preferred_element_type=jnp.float32
        ).astype(jnp.bfloat16)
        return picked.reshape(block_count, rand_count, head_count, block_len, head_dim)

    far_keys = fetch(kv_pairs[0])
    far_vals = fetch(kv_pairs[1])
    pair_view = padded.reshape(block_count + 2, block_len, 2, head_count, head_dim)
    window_pairs = jnp.stack(
        [pair_view[:block_count], pair_view[1 : block_count + 1], pair_view[2:]], axis=1
    ).reshape(block_count, 3 * block_len, 2, head_count, head_dim)
    window_keys = window_pairs[:, :, 0]
    window_vals = window_pairs[:, :, 1]
    first_pairs = first_block.reshape(block_len, 2, head_count, head_dim)
    first_keys = first_pairs[:, 0]
    first_vals = first_pairs[:, 1]
    global_ids = seq_index * block_count + jnp.arange(block_count, dtype=jnp.int32)
    block_total = seq_count * block_count
    window_live = jnp.stack([global_ids > 0, global_ids >= 0, global_ids < block_total - 1], axis=1)
    window_mask = jnp.repeat(window_live, block_len, axis=1)[None, :, None, :]
    query_blocks = q_rows.reshape(block_count, block_len, head_count, head_dim)
    softmax_scale = 1.0 / math.sqrt(head_dim)
    score_window = (
        jnp.einsum("ibhd,ikhd->hibk", query_blocks, window_keys, preferred_element_type=jnp.float32)
        * softmax_scale
    )
    score_first = (
        jnp.einsum("ibhd,khd->hibk", query_blocks, first_keys, preferred_element_type=jnp.float32)
        * softmax_scale
    )
    score_far = (
        jnp.einsum("ibhd,irhtd->hibrt", query_blocks, far_keys, preferred_element_type=jnp.float32)
        * softmax_scale
    )
    max_window = jnp.max(jnp.where(window_mask, score_window, -jnp.inf), axis=-1, keepdims=True)
    max_first = jnp.max(score_first, axis=-1, keepdims=True)
    max_far = jnp.max(score_far, axis=(-2, -1))[..., None]
    row_max = jnp.maximum(jnp.maximum(max_window, max_first), max_far)
    weight_window = jnp.where(window_mask, jnp.exp(score_window - row_max), 0.0)
    weight_first = jnp.exp(score_first - row_max)
    weight_far = jnp.exp(score_far - row_max[..., None])
    totals = (
        jnp.sum(weight_window, axis=-1, keepdims=True)
        + jnp.sum(weight_first, axis=-1, keepdims=True)
        + jnp.sum(weight_far, axis=(-2, -1))[..., None]
    )
    mixed = jnp.einsum(
        "hibk,ikhd->ibhd",
        weight_window.astype(jnp.bfloat16),
        window_vals,
        preferred_element_type=jnp.float32,
    )
    mixed = mixed + jnp.einsum(
        "hibk,khd->ibhd",
        weight_first.astype(jnp.bfloat16),
        first_vals,
        preferred_element_type=jnp.float32,
    )
    mixed = mixed + jnp.einsum(
        "hibrt,irhtd->ibhd",
        weight_far.astype(jnp.bfloat16),
        far_vals,
        preferred_element_type=jnp.float32,
    )
    totals_rows = jnp.transpose(totals, (1, 2, 0, 3))
    attn = (mixed / totals_rows).astype(jnp.bfloat16)
    logsum = row_max + jnp.log(totals)
    attn_rows = attn.reshape(shard_len, width_cols)
    layer_out = lax.psum_scatter(
        jnp.dot(attn_rows, out_weight, preferred_element_type=jnp.float32),
        "head",
        scatter_dimension=0,
        tiled=True,
    ).astype(jnp.bfloat16)[None]
    piece_flat = lax.all_gather(cotangent, "head", axis=1, tiled=True)[0]
    grad_piece = jnp.dot(piece_flat, out_weight.T, preferred_element_type=jnp.float32).astype(
        jnp.bfloat16
    )
    weight_acc = jnp.dot(attn_rows.T, piece_flat, preferred_element_type=jnp.float32)
    token_total = lax.axis_size("dp") * seq_count * shard_len
    dp_index = lax.axis_index("dp")
    half_rows = width_cols // 2
    mine = lax.dynamic_slice_in_dim(weight_acc, dp_index * half_rows, half_rows, axis=0)
    theirs = lax.dynamic_slice_in_dim(weight_acc, (1 - dp_index) * half_rows, half_rows, axis=0)
    mine = mine + lax.ppermute(theirs, "dp", [(0, 1), (1, 0)])
    mine = lax.psum(mine, "seq") * (1.0 / math.sqrt(token_total))
    other = lax.ppermute(mine, "dp", [(0, 1), (1, 0)])
    weight_grad = jnp.where(
        dp_index == 0,
        jnp.concatenate([mine, other], axis=0),
        jnp.concatenate([other, mine], axis=0),
    )
    grad_blocks = grad_piece.reshape(block_count, block_len, head_count, head_dim)
    delta_rows = jnp.sum(grad_blocks.astype(jnp.float32) * attn.astype(jnp.float32), axis=-1)
    row_delta = jnp.transpose(delta_rows, (2, 0, 1))[..., None]
    prob_window = jnp.where(window_mask, jnp.exp(score_window - logsum), 0.0)
    prob_first = jnp.exp(score_first - logsum)
    prob_far = jnp.exp(score_far - logsum[..., None])
    dprob_window = jnp.einsum(
        "ibhd,ikhd->hibk", grad_blocks, window_vals, preferred_element_type=jnp.float32
    )
    dprob_first = jnp.einsum(
        "ibhd,khd->hibk", grad_blocks, first_vals, preferred_element_type=jnp.float32
    )
    dprob_far = jnp.einsum(
        "ibhd,irhtd->hibrt", grad_blocks, far_vals, preferred_element_type=jnp.float32
    )
    dscore_window = (prob_window * (dprob_window - row_delta)).astype(jnp.bfloat16)
    dscore_first = (prob_first * (dprob_first - row_delta)).astype(jnp.bfloat16)
    dscore_far = (prob_far * (dprob_far - row_delta[..., None])).astype(jnp.bfloat16)
    grad_q = jnp.einsum(
        "hibk,ikhd->ibhd", dscore_window, window_keys, preferred_element_type=jnp.float32
    )
    grad_q = grad_q + jnp.einsum(
        "hibk,khd->ibhd", dscore_first, first_keys, preferred_element_type=jnp.float32
    )
    grad_q = grad_q + jnp.einsum(
        "hibrt,irhtd->ibhd", dscore_far, far_keys, preferred_element_type=jnp.float32
    )
    grad_q = (grad_q * softmax_scale).astype(jnp.bfloat16)
    key_window = (
        jnp.einsum(
            "hibk,ibhd->ikhd", dscore_window, query_blocks, preferred_element_type=jnp.float32
        )
        * softmax_scale
    )
    value_window = jnp.einsum(
        "hibk,ibhd->ikhd",
        prob_window.astype(jnp.bfloat16),
        grad_blocks,
        preferred_element_type=jnp.float32,
    )
    key_first = (
        jnp.einsum("hibk,ibhd->khd", dscore_first, query_blocks, preferred_element_type=jnp.float32)
        * softmax_scale
    )
    value_first = jnp.einsum(
        "hibk,ibhd->khd",
        prob_first.astype(jnp.bfloat16),
        grad_blocks,
        preferred_element_type=jnp.float32,
    )
    key_far = (
        jnp.einsum(
            "hibrt,ibhd->irhtd", dscore_far, query_blocks, preferred_element_type=jnp.float32
        )
        * softmax_scale
    )
    value_far = jnp.einsum(
        "hibrt,ibhd->irhtd",
        prob_far.astype(jnp.bfloat16),
        grad_blocks,
        preferred_element_type=jnp.float32,
    )
    window_terms = jnp.stack(
        [
            key_window.reshape(block_count, 3, block_len, head_count, head_dim),
            value_window.reshape(block_count, 3, block_len, head_count, head_dim),
        ],
        axis=3,
    )
    grad_pad = jnp.zeros((block_count + 2, block_len, 2, head_count, head_dim), jnp.float32)
    grad_pad = (
        grad_pad.at[:block_count]
        .add(window_terms[:, 0])
        .at[1 : block_count + 1]
        .add(window_terms[:, 1])
        .at[2:]
        .add(window_terms[:, 2])
    )
    global_grad = reduce_to_first(
        jnp.stack([key_first, value_first], axis=1).reshape(block_len, 2 * width_cols), "seq"
    ).reshape(block_len, 2, head_count, head_dim)
    grad_pad = grad_pad.at[1].add(jnp.where(seq_index == 0, global_grad, 0.0))
    rims = jnp.concatenate([grad_pad[0], grad_pad[block_count + 1]], axis=0).reshape(
        2 * block_len, 2 * width_cols
    )
    rim_sums = with_halo(rims.astype(jnp.bfloat16), (("seq", 0),), block_len).astype(rims.dtype)
    core = grad_pad[1 : block_count + 1].reshape(shard_len, 2 * width_cols)
    core = (
        core.at[:block_len]
        .add(rim_sums[:block_len])
        .at[shard_len - block_len :]
        .add(rim_sums[3 * block_len :])
    )
    core = core.reshape(block_count, block_len, 2, head_count, head_dim)
    def give_back(terms):
        terms = terms.reshape(request_count, block_len * head_dim).astype(jnp.bfloat16)
        outgoing = jnp.dot(pick_hot.T, terms, preferred_element_type=jnp.float32).astype(
            jnp.bfloat16
        )
        outgoing = outgoing.reshape(seq_count, capacity, block_len, head_dim)
        incoming = lax.all_to_all(outgoing, "seq", split_axis=0, concat_axis=0, tiled=True)
        return jnp.dot(
            serve_hot.T, incoming.reshape(slot_total, -1), preferred_element_type=jnp.float32
        ).reshape(block_count, head_count, block_len, head_dim)

    added_vals = give_back(value_far)
    added_keys = give_back(key_far)
    added = jnp.stack([added_keys, added_vals], axis=3)
    core = core + jnp.transpose(added, (0, 2, 3, 1, 4))
    grad_k = core[:, :, 0].reshape(shard_len, width_cols).astype(jnp.bfloat16)
    grad_v = core[:, :, 1].reshape(shard_len, width_cols).astype(jnp.bfloat16)
    grad_q_rows = grad_q.reshape(shard_len, width_cols)
    head_index = lax.axis_index("head")

    def to_owners(rows):
        count = rows.shape[0]
        rows = rows.reshape(count, group_count, piece_len, width_cols)
        pieces = [lax.dynamic_index_in_dim(rows, head_index, axis=1, keepdims=False)]
        for shift in range(1, group_count):
            pairs = [(i, (i + shift) % group_count) for i in range(group_count)]
            sent = lax.dynamic_index_in_dim(
                rows, (head_index + shift) % group_count, axis=1, keepdims=False
            )
            pieces.append(lax.ppermute(sent, "head", pairs))
        pieces = jnp.stack(pieces)
        order = (head_index - jnp.arange(group_count, dtype=jnp.int32)) % group_count
        pieces = jnp.take(pieces, order, axis=0)
        return jnp.transpose(pieces, (1, 2, 0, 3)).reshape(
            count, 1, piece_len, group_count * width_cols
        )

    grad_queries = to_owners(grad_q_rows[None])[0]
    back = to_owners(jnp.stack([grad_k, grad_v]))
    grad_keys, grad_values = back[0], back[1]
    return (layer_out, grad_queries, grad_keys, grad_values, weight_grad)


def solution(mesh):
    in_specs = (
        P("dp", ("seq", "head"), None),
        P("dp", ("seq", "head"), None),
        P("dp", ("seq", "head"), None),
        P("seq", "head", None),
        P("head", None),
        P("dp", ("seq", "head"), None),
    )
    out_specs = (
        P("dp", ("seq", "head"), None),
        P("dp", ("seq", "head"), None),
        P("dp", ("seq", "head"), None),
        P("dp", ("seq", "head"), None),
        P("head", None),
    )
    return jax.shard_map(
        per_device, mesh=mesh, in_specs=in_specs, out_specs=out_specs, check_vma=False
    )
```

```python
import math

import jax
import jax.numpy as jnp
from jax import lax
from jax.sharding import PartitionSpec as P

HEAD_SIZE = 128
BLOCK_TOKENS = 64


def with_halo(block, sides, width):
    for axis, dim in sides:
        count = lax.axis_size(axis)
        forward = [(i, i + 1) for i in range(count - 1)]
        backward = [(target, source) for source, target in forward]
        low = lax.ppermute(
            lax.slice_in_dim(block, block.shape[dim] - width, None, axis=dim), axis, forward
        )
        high = lax.ppermute(lax.slice_in_dim(block, 0, width, axis=dim), axis, backward)
        block = jnp.concatenate([low, block, high], axis=dim)
    return block


def broadcast_first(block, axis, radix=4):
    count = lax.axis_size(axis)
    index = lax.axis_index(axis)
    stride = 1
    while stride * radix < count:
        stride *= radix
    while stride >= 1:
        span = stride * radix
        updated = block
        for m in range(1, radix):
            pairs = [(j, j + m * stride) for j in range(0, count, span) if j + m * stride < count]
            if pairs:
                got = lax.ppermute(block, axis, pairs)
                updated = jnp.where(index % span == m * stride, got, updated)
        block = updated
        stride //= radix
    return block


def reduce_to_first(block, axis, radix=4):
    count = lax.axis_size(axis)
    stride = 1
    while stride < count:
        span = stride * radix
        total = block
        for m in range(1, radix):
            pairs = [(j + m * stride, j) for j in range(0, count, span) if j + m * stride < count]
            if pairs:
                total = total + lax.ppermute(block, axis, pairs)
        block = total
        stride *= radix
    return block


def request_slots(rand_blocks, block_count, head_count, seq_count, capacity):
    requests = jnp.transpose(rand_blocks, (0, 2, 1)).reshape(-1)
    head_of = jnp.arange(requests.shape[0], dtype=jnp.int32) % head_count
    owners = requests // block_count
    offsets = requests % block_count
    one_hot = (owners[:, None] == jnp.arange(seq_count, dtype=jnp.int32)[None, :]).astype(
        jnp.bfloat16
    )
    count = requests.shape[0]
    lower = (
        jnp.arange(count, dtype=jnp.int32)[:, None] >= jnp.arange(count, dtype=jnp.int32)[None, :]
    ).astype(jnp.bfloat16)
    running = jnp.dot(lower, one_hot, preferred_element_type=jnp.float32)
    position = jnp.sum(one_hot.astype(jnp.float32) * (running - 1.0), axis=1).astype(jnp.int32)
    return owners, position, offsets * head_count + head_of


def gather_all(block, axis, radix=4):
    count = lax.axis_size(axis)
    if count != radix * radix:
        return lax.all_gather(block, axis, axis=0, tiled=False)
    index = lax.axis_index(axis)
    for stride in (1, radix):
        place = (index // stride) % radix
        pieces = [block]
        for m in range(1, radix):
            pairs = [
                (i, i - ((i // stride) % radix) * stride + (((i // stride) % radix + m) % radix) * stride)
                for i in range(count)
            ]
            pieces.append(lax.ppermute(block, axis, pairs))
        pieces = jnp.stack(pieces)
        order = (place - jnp.arange(radix, dtype=jnp.int32)) % radix
        block = jnp.take(pieces, order, axis=0)
        if stride > 1:
            block = block.reshape((radix * radix,) + block.shape[2:])
    return block


def per_device(queries, key_rows, values, rand_blocks, out_weight, cotangent):
    block_len = BLOCK_TOKENS
    head_dim = HEAD_SIZE
    seq_count = lax.axis_size("seq")
    seq_index = lax.axis_index("seq")
    group_count = lax.axis_size("head")
    piece_len = queries.shape[1]
    width_cols = queries.shape[2] // group_count
    stacked = jnp.concatenate([queries, key_rows, values], axis=0)
    stacked = jnp.transpose(stacked.reshape(3, piece_len, group_count, width_cols), (2, 0, 1, 3))
    stacked = lax.all_to_all(stacked, "head", split_axis=0, concat_axis=0, tiled=True)
    stacked = jnp.transpose(stacked, (1, 0, 2, 3)).reshape(3, group_count * piece_len, width_cols)
    q_rows = stacked[0]
    shard_len = q_rows.shape[0]
    head_count = width_cols // head_dim
    block_count = shard_len // block_len
    rand_count = rand_blocks.shape[2]
    key_value = jnp.concatenate([stacked[1], stacked[2]], axis=1)
    padded = with_halo(key_value, (("seq", 0),), block_len)
    first_block = broadcast_first(key_value[:block_len], "seq")
    request_count = rand_blocks.shape[0] * rand_blocks.shape[1] * rand_blocks.shape[2]
    capacity = 3 * request_count // (2 * seq_count)
    owners, position, codes = request_slots(
        rand_blocks, block_count, head_count, seq_count, capacity
    )
    slot_of = owners * capacity + position
    every_block = gather_all(rand_blocks, "seq")
    all_owners, all_position, all_codes = jax.vmap(
        lambda r: request_slots(r, block_count, head_count, seq_count, capacity)
    )(every_block)
    match = (all_owners[:, :, None] == seq_index) & (
        all_position[:, :, None] == jnp.arange(capacity, dtype=jnp.int32)[None, None, :]
    )
    asked_here = jnp.sum(jnp.where(match, all_codes[:, :, None] + 1, 0), axis=1) - 1
    slot_total = seq_count * capacity
    pair_count = block_count * head_count
    asked_flat = asked_here.reshape(slot_total)
    serve_hot = (
        asked_flat[:, None] == jnp.arange(pair_count, dtype=jnp.int32)[None, :]
    ).astype(jnp.bfloat16)
    pick_hot = (
        slot_of[:, None] == jnp.arange(slot_total, dtype=jnp.int32)[None, :]
    ).astype(jnp.bfloat16)
    kv_pairs = jnp.transpose(
        key_value.reshape(block_count, block_len, 2, head_count, head_dim), (2, 0, 3, 1, 4)
    ).reshape(2, pair_count, block_len * head_dim)

    def fetch(pairs):
        served = jnp.dot(serve_hot, pairs, preferred_element_type=jnp.float32).astype(jnp.bfloat16)
        served = served.reshape(seq_count, capacity, block_len, head_dim)
        received = lax.all_to_all(served, "seq", split_axis=0, concat_axis=0, tiled=True)
        picked = jnp.dot(
            pick_hot, received.reshape(slot_total, -1), preferred_element_type=jnp.float32
        ).astype(jnp.bfloat16)
        return picked.reshape(block_count, rand_count, head_count, block_len, head_dim)

    far_keys = fetch(kv_pairs[0])
    far_vals = fetch(kv_pairs[1])
    pair_view = padded.reshape(block_count + 2, block_len, 2, head_count, head_dim)
    window_pairs = jnp.stack(
        [pair_view[:block_count], pair_view[1 : block_count + 1], pair_view[2:]], axis=1
    ).reshape(block_count, 3 * block_len, 2, head_count, head_dim)
    window_keys = window_pairs[:, :, 0]
    window_vals = window_pairs[:, :, 1]
    first_pairs = first_block.reshape(block_len, 2, head_count, head_dim)
    first_keys = first_pairs[:, 0]
    first_vals = first_pairs[:, 1]
    global_ids = seq_index * block_count + jnp.arange(block_count, dtype=jnp.int32)
    block_total = seq_count * block_count
    window_live = jnp.stack([global_ids > 0, global_ids >= 0, global_ids < block_total - 1], axis=1)
    window_mask = jnp.repeat(window_live, block_len, axis=1)[None, :, None, :]
    query_blocks = q_rows.reshape(block_count, block_len, head_count, head_dim)
    softmax_scale = 1.0 / math.sqrt(head_dim)
    score_window = (
        jnp.einsum("ibhd,ikhd->hibk", query_blocks, window_keys, preferred_element_type=jnp.float32)
        * softmax_scale
    )
    score_first = (
        jnp.einsum("ibhd,khd->hibk", query_blocks, first_keys, preferred_element_type=jnp.float32)
        * softmax_scale
    )
    score_far = (
        jnp.einsum("ibhd,irhtd->hibrt", query_blocks, far_keys, preferred_element_type=jnp.float32)
        * softmax_scale
    )
    max_window = jnp.max(jnp.where(window_mask, score_window, -jnp.inf), axis=-1, keepdims=True)
    max_first = jnp.max(score_first, axis=-1, keepdims=True)
    max_far = jnp.max(score_far, axis=(-2, -1))[..., None]
    row_max = jnp.maximum(jnp.maximum(max_window, max_first), max_far)
    weight_window = jnp.where(window_mask, jnp.exp(score_window - row_max), 0.0)
    weight_first = jnp.exp(score_first - row_max)
    weight_far = jnp.exp(score_far - row_max[..., None])
    totals = (
        jnp.sum(weight_window, axis=-1, keepdims=True)
        + jnp.sum(weight_first, axis=-1, keepdims=True)
        + jnp.sum(weight_far, axis=(-2, -1))[..., None]
    )
    mixed = jnp.einsum(
        "hibk,ikhd->ibhd",
        weight_window.astype(jnp.bfloat16),
        window_vals,
        preferred_element_type=jnp.float32,
    )
    mixed = mixed + jnp.einsum(
        "hibk,khd->ibhd",
        weight_first.astype(jnp.bfloat16),
        first_vals,
        preferred_element_type=jnp.float32,
    )
    mixed = mixed + jnp.einsum(
        "hibrt,irhtd->ibhd",
        weight_far.astype(jnp.bfloat16),
        far_vals,
        preferred_element_type=jnp.float32,
    )
    totals_rows = jnp.transpose(totals, (1, 2, 0, 3))
    attn = (mixed / totals_rows).astype(jnp.bfloat16)
    logsum = row_max + jnp.log(totals)
    attn_rows = attn.reshape(shard_len, width_cols)
    layer_out = lax.psum_scatter(
        jnp.dot(attn_rows, out_weight, preferred_element_type=jnp.float32).astype(jnp.bfloat16),
        "head",
        scatter_dimension=0,
        tiled=True,
    )[None]
    piece_flat = lax.all_gather(cotangent, "head", axis=1, tiled=True)[0]
    grad_piece = jnp.dot(piece_flat, out_weight.T, preferred_element_type=jnp.float32).astype(
        jnp.bfloat16
    )
    weight_acc = jnp.dot(attn_rows.T, piece_flat, preferred_element_type=jnp.float32)
    token_total = lax.axis_size("dp") * seq_count * shard_len
    dp_index = lax.axis_index("dp")
    half_rows = width_cols // 2
    mine = lax.dynamic_slice_in_dim(weight_acc, dp_index * half_rows, half_rows, axis=0)
    theirs = lax.dynamic_slice_in_dim(weight_acc, (1 - dp_index) * half_rows, half_rows, axis=0)
    mine = mine + lax.ppermute(theirs, "dp", [(0, 1), (1, 0)])
    mine = lax.psum(mine.astype(jnp.bfloat16), "seq").astype(jnp.float32) * (
        1.0 / math.sqrt(token_total)
    )
    other = lax.ppermute(mine, "dp", [(0, 1), (1, 0)])
    weight_grad = jnp.where(
        dp_index == 0,
        jnp.concatenate([mine, other], axis=0),
        jnp.concatenate([other, mine], axis=0),
    )
    grad_blocks = grad_piece.reshape(block_count, block_len, head_count, head_dim)
    delta_rows = jnp.sum(grad_blocks.astype(jnp.float32) * attn.astype(jnp.float32), axis=-1)
    row_delta = jnp.transpose(delta_rows, (2, 0, 1))[..., None]
    prob_window = jnp.where(window_mask, jnp.exp(score_window - logsum), 0.0)
    prob_first = jnp.exp(score_first - logsum)
    prob_far = jnp.exp(score_far - logsum[..., None])
    dprob_window = jnp.einsum(
        "ibhd,ikhd->hibk", grad_blocks, window_vals, preferred_element_type=jnp.float32
    )
    dprob_first = jnp.einsum(
        "ibhd,khd->hibk", grad_blocks, first_vals, preferred_element_type=jnp.float32
    )
    dprob_far = jnp.einsum(
        "ibhd,irhtd->hibrt", grad_blocks, far_vals, preferred_element_type=jnp.float32
    )
    dscore_window = (prob_window * (dprob_window - row_delta)).astype(jnp.bfloat16)
    dscore_first = (prob_first * (dprob_first - row_delta)).astype(jnp.bfloat16)
    dscore_far = (prob_far * (dprob_far - row_delta[..., None])).astype(jnp.bfloat16)
    grad_q = jnp.einsum(
        "hibk,ikhd->ibhd", dscore_window, window_keys, preferred_element_type=jnp.float32
    )
    grad_q = grad_q + jnp.einsum(
        "hibk,khd->ibhd", dscore_first, first_keys, preferred_element_type=jnp.float32
    )
    grad_q = grad_q + jnp.einsum(
        "hibrt,irhtd->ibhd", dscore_far, far_keys, preferred_element_type=jnp.float32
    )
    grad_q = (grad_q * softmax_scale).astype(jnp.bfloat16)
    key_window = (
        jnp.einsum(
            "hibk,ibhd->ikhd", dscore_window, query_blocks, preferred_element_type=jnp.float32
        )
        * softmax_scale
    )
    value_window = jnp.einsum(
        "hibk,ibhd->ikhd",
        prob_window.astype(jnp.bfloat16),
        grad_blocks,
        preferred_element_type=jnp.float32,
    )
    key_first = (
        jnp.einsum("hibk,ibhd->khd", dscore_first, query_blocks, preferred_element_type=jnp.float32)
        * softmax_scale
    )
    value_first = jnp.einsum(
        "hibk,ibhd->khd",
        prob_first.astype(jnp.bfloat16),
        grad_blocks,
        preferred_element_type=jnp.float32,
    )
    key_far = (
        jnp.einsum(
            "hibrt,ibhd->irhtd", dscore_far, query_blocks, preferred_element_type=jnp.float32
        )
        * softmax_scale
    )
    value_far = jnp.einsum(
        "hibrt,ibhd->irhtd",
        prob_far.astype(jnp.bfloat16),
        grad_blocks,
        preferred_element_type=jnp.float32,
    )
    window_terms = jnp.stack(
        [
            key_window.reshape(block_count, 3, block_len, head_count, head_dim),
            value_window.reshape(block_count, 3, block_len, head_count, head_dim),
        ],
        axis=3,
    )
    grad_pad = jnp.zeros((block_count + 2, block_len, 2, head_count, head_dim), jnp.float32)
    grad_pad = (
        grad_pad.at[:block_count]
        .add(window_terms[:, 0])
        .at[1 : block_count + 1]
        .add(window_terms[:, 1])
        .at[2:]
        .add(window_terms[:, 2])
    )
    global_grad = reduce_to_first(
        jnp.stack([key_first, value_first], axis=1).reshape(block_len, 2 * width_cols), "seq"
    ).reshape(block_len, 2, head_count, head_dim)
    grad_pad = grad_pad.at[1].add(jnp.where(seq_index == 0, global_grad, 0.0))
    rims = jnp.concatenate([grad_pad[0], grad_pad[block_count + 1]], axis=0).reshape(
        2 * block_len, 2 * width_cols
    )
    rim_sums = with_halo(rims.astype(jnp.bfloat16), (("seq", 0),), block_len).astype(rims.dtype)
    core = grad_pad[1 : block_count + 1].reshape(shard_len, 2 * width_cols)
    core = (
        core.at[:block_len]
        .add(rim_sums[:block_len])
        .at[shard_len - block_len :]
        .add(rim_sums[3 * block_len :])
    )
    core = core.reshape(block_count, block_len, 2, head_count, head_dim)
    def give_back(terms):
        terms = terms.reshape(request_count, block_len * head_dim).astype(jnp.bfloat16)
        outgoing = jnp.dot(pick_hot.T, terms, preferred_element_type=jnp.float32).astype(
            jnp.bfloat16
        )
        outgoing = outgoing.reshape(seq_count, capacity, block_len, head_dim)
        incoming = lax.all_to_all(outgoing, "seq", split_axis=0, concat_axis=0, tiled=True)
        return jnp.dot(
            serve_hot.T, incoming.reshape(slot_total, -1), preferred_element_type=jnp.float32
        ).reshape(block_count, head_count, block_len, head_dim)

    added_vals = give_back(value_far)
    added_keys = give_back(key_far)
    added = jnp.stack([added_keys, added_vals], axis=3)
    core = core + jnp.transpose(added, (0, 2, 3, 1, 4))
    grad_k = core[:, :, 0].reshape(shard_len, width_cols).astype(jnp.bfloat16)
    grad_v = core[:, :, 1].reshape(shard_len, width_cols).astype(jnp.bfloat16)
    grad_q_rows = grad_q.reshape(shard_len, width_cols)
    head_index = lax.axis_index("head")

    def to_owners(rows):
        count = rows.shape[0]
        rows = rows.reshape(count, group_count, piece_len, width_cols)
        pieces = [lax.dynamic_index_in_dim(rows, head_index, axis=1, keepdims=False)]
        for shift in range(1, group_count):
            pairs = [(i, (i + shift) % group_count) for i in range(group_count)]
            sent = lax.dynamic_index_in_dim(
                rows, (head_index + shift) % group_count, axis=1, keepdims=False
            )
            pieces.append(lax.ppermute(sent, "head", pairs))
        pieces = jnp.stack(pieces)
        order = (head_index - jnp.arange(group_count, dtype=jnp.int32)) % group_count
        pieces = jnp.take(pieces, order, axis=0)
        return jnp.transpose(pieces, (1, 2, 0, 3)).reshape(
            count, 1, piece_len, group_count * width_cols
        )

    grad_queries = to_owners(grad_q_rows[None])[0]
    back = to_owners(jnp.stack([grad_k, grad_v]))
    grad_keys, grad_values = back[0], back[1]
    return (layer_out, grad_queries, grad_keys, grad_values, weight_grad)


def solution(mesh):
    in_specs = (
        P("dp", ("seq", "head"), None),
        P("dp", ("seq", "head"), None),
        P("dp", ("seq", "head"), None),
        P("seq", "head", None),
        P("head", None),
        P("dp", ("seq", "head"), None),
    )
    out_specs = (
        P("dp", ("seq", "head"), None),
        P("dp", ("seq", "head"), None),
        P("dp", ("seq", "head"), None),
        P("dp", ("seq", "head"), None),
        P("head", None),
    )
    return jax.shard_map(
        per_device, mesh=mesh, in_specs=in_specs, out_specs=out_specs, check_vma=False
    )
```

```python
import math

import jax
import jax.numpy as jnp
from jax import lax
from jax.sharding import PartitionSpec as P

HEAD_SIZE = 128
BLOCK_TOKENS = 64


def with_halo(block, sides, width):
    for axis, dim in sides:
        count = lax.axis_size(axis)
        forward = [(i, i + 1) for i in range(count - 1)]
        backward = [(target, source) for source, target in forward]
        low = lax.ppermute(
            lax.slice_in_dim(block, block.shape[dim] - width, None, axis=dim), axis, forward
        )
        high = lax.ppermute(lax.slice_in_dim(block, 0, width, axis=dim), axis, backward)
        block = jnp.concatenate([low, block, high], axis=dim)
    return block


def broadcast_first(block, axis, radix=4):
    count = lax.axis_size(axis)
    index = lax.axis_index(axis)
    stride = 1
    while stride * radix < count:
        stride *= radix
    while stride >= 1:
        span = stride * radix
        updated = block
        for m in range(1, radix):
            pairs = [(j, j + m * stride) for j in range(0, count, span) if j + m * stride < count]
            if pairs:
                got = lax.ppermute(block, axis, pairs)
                updated = jnp.where(index % span == m * stride, got, updated)
        block = updated
        stride //= radix
    return block


def reduce_to_first(block, axis, radix=4):
    count = lax.axis_size(axis)
    stride = 1
    while stride < count:
        span = stride * radix
        total = block
        for m in range(1, radix):
            pairs = [(j + m * stride, j) for j in range(0, count, span) if j + m * stride < count]
            if pairs:
                total = total + lax.ppermute(block, axis, pairs)
        block = total
        stride *= radix
    return block


def request_slots(rand_blocks, block_count, head_count, seq_count, capacity):
    requests = jnp.transpose(rand_blocks, (0, 2, 1)).reshape(-1)
    head_of = jnp.arange(requests.shape[0], dtype=jnp.int32) % head_count
    owners = requests // block_count
    offsets = requests % block_count
    one_hot = (owners[:, None] == jnp.arange(seq_count, dtype=jnp.int32)[None, :]).astype(
        jnp.bfloat16
    )
    count = requests.shape[0]
    lower = (
        jnp.arange(count, dtype=jnp.int32)[:, None] >= jnp.arange(count, dtype=jnp.int32)[None, :]
    ).astype(jnp.bfloat16)
    running = jnp.dot(lower, one_hot, preferred_element_type=jnp.float32)
    position = jnp.sum(one_hot.astype(jnp.float32) * (running - 1.0), axis=1).astype(jnp.int32)
    return owners, position, offsets * head_count + head_of


def gather_all(block, axis, radix=4):
    count = lax.axis_size(axis)
    if count != radix * radix:
        return lax.all_gather(block, axis, axis=0, tiled=False)
    index = lax.axis_index(axis)
    for stride in (1, radix):
        place = (index // stride) % radix
        pieces = [block]
        for m in range(1, radix):
            pairs = [
                (i, i - ((i // stride) % radix) * stride + (((i // stride) % radix + m) % radix) * stride)
                for i in range(count)
            ]
            pieces.append(lax.ppermute(block, axis, pairs))
        pieces = jnp.stack(pieces)
        order = (place - jnp.arange(radix, dtype=jnp.int32)) % radix
        block = jnp.take(pieces, order, axis=0)
        if stride > 1:
            block = block.reshape((radix * radix,) + block.shape[2:])
    return block


def per_device(queries, key_rows, values, rand_blocks, out_weight, cotangent):
    block_len = BLOCK_TOKENS
    head_dim = HEAD_SIZE
    seq_count = lax.axis_size("seq")
    seq_index = lax.axis_index("seq")
    group_count = lax.axis_size("head")
    piece_len = queries.shape[1]
    width_cols = queries.shape[2] // group_count
    head_index = lax.axis_index("head")

    def from_owners(rows):
        count = rows.shape[0]
        rows = rows.reshape(count, piece_len, group_count, width_cols)
        pieces = [lax.dynamic_index_in_dim(rows, head_index, axis=2, keepdims=False)]
        for shift in range(1, group_count):
            pairs = [(i, (i + shift) % group_count) for i in range(group_count)]
            sent = lax.dynamic_index_in_dim(
                rows, (head_index + shift) % group_count, axis=2, keepdims=False
            )
            pieces.append(lax.ppermute(sent, "head", pairs))
        pieces = jnp.stack(pieces)
        order = (head_index - jnp.arange(group_count, dtype=jnp.int32)) % group_count
        pieces = jnp.take(pieces, order, axis=0)
        return jnp.transpose(pieces, (1, 0, 2, 3)).reshape(count, group_count * piece_len, width_cols)

    k_rows = from_owners(key_rows)[0]
    v_rows = from_owners(values)[0]
    q_rows = from_owners(queries)[0]
    shard_len = q_rows.shape[0]
    head_count = width_cols // head_dim
    block_count = shard_len // block_len
    rand_count = rand_blocks.shape[2]
    key_value = jnp.concatenate([k_rows, v_rows], axis=1)
    padded = with_halo(key_value, (("seq", 0),), block_len)
    first_block = broadcast_first(key_value[:block_len], "seq")
    request_count = rand_blocks.shape[0] * rand_blocks.shape[1] * rand_blocks.shape[2]
    capacity = 3 * request_count // (2 * seq_count)
    owners, position, codes = request_slots(
        rand_blocks, block_count, head_count, seq_count, capacity
    )
    slot_of = owners * capacity + position
    every_block = gather_all(rand_blocks, "seq")
    all_owners, all_position, all_codes = jax.vmap(
        lambda r: request_slots(r, block_count, head_count, seq_count, capacity)
    )(every_block)
    match = (all_owners[:, :, None] == seq_index) & (
        all_position[:, :, None] == jnp.arange(capacity, dtype=jnp.int32)[None, None, :]
    )
    asked_here = jnp.sum(jnp.where(match, all_codes[:, :, None] + 1, 0), axis=1) - 1
    slot_total = seq_count * capacity
    pair_count = block_count * head_count
    asked_flat = asked_here.reshape(slot_total)
    serve_hot = (
        asked_flat[:, None] == jnp.arange(pair_count, dtype=jnp.int32)[None, :]
    ).astype(jnp.bfloat16)
    pick_hot = (
        slot_of[:, None] == jnp.arange(slot_total, dtype=jnp.int32)[None, :]
    ).astype(jnp.bfloat16)
    kv_pairs = jnp.transpose(
        key_value.reshape(block_count, block_len, 2, head_count, head_dim), (2, 0, 3, 1, 4)
    ).reshape(2, pair_count, block_len * head_dim)

    def fetch(pairs):
        served = jnp.dot(serve_hot, pairs, preferred_element_type=jnp.float32).astype(jnp.bfloat16)
        served = served.reshape(seq_count, capacity, block_len, head_dim)
        received = lax.all_to_all(served, "seq", split_axis=0, concat_axis=0, tiled=True)
        picked = jnp.dot(
            pick_hot, received.reshape(slot_total, -1), preferred_element_type=jnp.float32
        ).astype(jnp.bfloat16)
        return picked.reshape(block_count, rand_count, head_count, block_len, head_dim)

    far_keys = fetch(kv_pairs[0])
    far_vals = fetch(kv_pairs[1])
    pair_view = padded.reshape(block_count + 2, block_len, 2, head_count, head_dim)
    window_pairs = jnp.stack(
        [pair_view[:block_count], pair_view[1 : block_count + 1], pair_view[2:]], axis=1
    ).reshape(block_count, 3 * block_len, 2, head_count, head_dim)
    window_keys = window_pairs[:, :, 0]
    window_vals = window_pairs[:, :, 1]
    first_pairs = first_block.reshape(block_len, 2, head_count, head_dim)
    first_keys = first_pairs[:, 0]
    first_vals = first_pairs[:, 1]
    global_ids = seq_index * block_count + jnp.arange(block_count, dtype=jnp.int32)
    block_total = seq_count * block_count
    window_live = jnp.stack([global_ids > 0, global_ids >= 0, global_ids < block_total - 1], axis=1)
    window_mask = jnp.repeat(window_live, block_len, axis=1)[None, :, None, :]
    query_blocks = q_rows.reshape(block_count, block_len, head_count, head_dim)
    softmax_scale = 1.0 / math.sqrt(head_dim)
    score_window = (
        jnp.einsum("ibhd,ikhd->hibk", query_blocks, window_keys, preferred_element_type=jnp.float32)
        * softmax_scale
    )
    score_first = (
        jnp.einsum("ibhd,khd->hibk", query_blocks, first_keys, preferred_element_type=jnp.float32)
        * softmax_scale
    )
    score_far = (
        jnp.einsum("ibhd,irhtd->hibrt", query_blocks, far_keys, preferred_element_type=jnp.float32)
        * softmax_scale
    )
    max_window = jnp.max(jnp.where(window_mask, score_window, -jnp.inf), axis=-1, keepdims=True)
    max_first = jnp.max(score_first, axis=-1, keepdims=True)
    max_far = jnp.max(score_far, axis=(-2, -1))[..., None]
    row_max = jnp.maximum(jnp.maximum(max_window, max_first), max_far)
    weight_window = jnp.where(window_mask, jnp.exp(score_window - row_max), 0.0)
    weight_first = jnp.exp(score_first - row_max)
    weight_far = jnp.exp(score_far - row_max[..., None])
    totals = (
        jnp.sum(weight_window, axis=-1, keepdims=True)
        + jnp.sum(weight_first, axis=-1, keepdims=True)
        + jnp.sum(weight_far, axis=(-2, -1))[..., None]
    )
    mixed = jnp.einsum(
        "hibk,ikhd->ibhd",
        weight_window.astype(jnp.bfloat16),
        window_vals,
        preferred_element_type=jnp.float32,
    )
    mixed = mixed + jnp.einsum(
        "hibk,khd->ibhd",
        weight_first.astype(jnp.bfloat16),
        first_vals,
        preferred_element_type=jnp.float32,
    )
    mixed = mixed + jnp.einsum(
        "hibrt,irhtd->ibhd",
        weight_far.astype(jnp.bfloat16),
        far_vals,
        preferred_element_type=jnp.float32,
    )
    totals_rows = jnp.transpose(totals, (1, 2, 0, 3))
    attn = (mixed / totals_rows).astype(jnp.bfloat16)
    logsum = row_max + jnp.log(totals)
    attn_rows = attn.reshape(shard_len, width_cols)
    layer_out = lax.psum_scatter(
        jnp.dot(attn_rows, out_weight, preferred_element_type=jnp.float32).astype(jnp.bfloat16),
        "head",
        scatter_dimension=0,
        tiled=True,
    )[None]
    piece_flat = lax.all_gather(cotangent, "head", axis=1, tiled=True)[0]
    grad_piece = jnp.dot(piece_flat, out_weight.T, preferred_element_type=jnp.float32).astype(
        jnp.bfloat16
    )
    weight_acc = jnp.dot(attn_rows.T, piece_flat, preferred_element_type=jnp.float32)
    token_total = lax.axis_size("dp") * seq_count * shard_len
    dp_index = lax.axis_index("dp")
    half_rows = width_cols // 2
    mine = lax.dynamic_slice_in_dim(weight_acc, dp_index * half_rows, half_rows, axis=0)
    theirs = lax.dynamic_slice_in_dim(weight_acc, (1 - dp_index) * half_rows, half_rows, axis=0)
    mine = mine + lax.ppermute(theirs, "dp", [(0, 1), (1, 0)])
    mine = lax.psum(mine.astype(jnp.bfloat16), "seq").astype(jnp.float32) * (
        1.0 / math.sqrt(token_total)
    )
    other = lax.ppermute(mine, "dp", [(0, 1), (1, 0)])
    weight_grad = jnp.where(
        dp_index == 0,
        jnp.concatenate([mine, other], axis=0),
        jnp.concatenate([other, mine], axis=0),
    )
    grad_blocks = grad_piece.reshape(block_count, block_len, head_count, head_dim)
    delta_rows = jnp.sum(grad_blocks.astype(jnp.float32) * attn.astype(jnp.float32), axis=-1)
    row_delta = jnp.transpose(delta_rows, (2, 0, 1))[..., None]
    prob_window = jnp.where(window_mask, jnp.exp(score_window - logsum), 0.0)
    prob_first = jnp.exp(score_first - logsum)
    prob_far = jnp.exp(score_far - logsum[..., None])
    dprob_window = jnp.einsum(
        "ibhd,ikhd->hibk", grad_blocks, window_vals, preferred_element_type=jnp.float32
    )
    dprob_first = jnp.einsum(
        "ibhd,khd->hibk", grad_blocks, first_vals, preferred_element_type=jnp.float32
    )
    dprob_far = jnp.einsum(
        "ibhd,irhtd->hibrt", grad_blocks, far_vals, preferred_element_type=jnp.float32
    )
    dscore_window = (prob_window * (dprob_window - row_delta)).astype(jnp.bfloat16)
    dscore_first = (prob_first * (dprob_first - row_delta)).astype(jnp.bfloat16)
    dscore_far = (prob_far * (dprob_far - row_delta[..., None])).astype(jnp.bfloat16)
    grad_q = jnp.einsum(
        "hibk,ikhd->ibhd", dscore_window, window_keys, preferred_element_type=jnp.float32
    )
    grad_q = grad_q + jnp.einsum(
        "hibk,khd->ibhd", dscore_first, first_keys, preferred_element_type=jnp.float32
    )
    grad_q = grad_q + jnp.einsum(
        "hibrt,irhtd->ibhd", dscore_far, far_keys, preferred_element_type=jnp.float32
    )
    grad_q = (grad_q * softmax_scale).astype(jnp.bfloat16)
    key_window = (
        jnp.einsum(
            "hibk,ibhd->ikhd", dscore_window, query_blocks, preferred_element_type=jnp.float32
        )
        * softmax_scale
    )
    value_window = jnp.einsum(
        "hibk,ibhd->ikhd",
        prob_window.astype(jnp.bfloat16),
        grad_blocks,
        preferred_element_type=jnp.float32,
    )
    key_first = (
        jnp.einsum("hibk,ibhd->khd", dscore_first, query_blocks, preferred_element_type=jnp.float32)
        * softmax_scale
    )
    value_first = jnp.einsum(
        "hibk,ibhd->khd",
        prob_first.astype(jnp.bfloat16),
        grad_blocks,
        preferred_element_type=jnp.float32,
    )
    key_far = (
        jnp.einsum(
            "hibrt,ibhd->irhtd", dscore_far, query_blocks, preferred_element_type=jnp.float32
        )
        * softmax_scale
    )
    value_far = jnp.einsum(
        "hibrt,ibhd->irhtd",
        prob_far.astype(jnp.bfloat16),
        grad_blocks,
        preferred_element_type=jnp.float32,
    )
    window_terms = jnp.stack(
        [
            key_window.reshape(block_count, 3, block_len, head_count, head_dim),
            value_window.reshape(block_count, 3, block_len, head_count, head_dim),
        ],
        axis=3,
    )
    grad_pad = jnp.zeros((block_count + 2, block_len, 2, head_count, head_dim), jnp.float32)
    grad_pad = (
        grad_pad.at[:block_count]
        .add(window_terms[:, 0])
        .at[1 : block_count + 1]
        .add(window_terms[:, 1])
        .at[2:]
        .add(window_terms[:, 2])
    )
    global_grad = reduce_to_first(
        jnp.stack([key_first, value_first], axis=1).reshape(block_len, 2 * width_cols), "seq"
    ).reshape(block_len, 2, head_count, head_dim)
    grad_pad = grad_pad.at[1].add(jnp.where(seq_index == 0, global_grad, 0.0))
    rims = jnp.concatenate([grad_pad[0], grad_pad[block_count + 1]], axis=0).reshape(
        2 * block_len, 2 * width_cols
    )
    rim_sums = with_halo(rims.astype(jnp.bfloat16), (("seq", 0),), block_len).astype(rims.dtype)
    core = grad_pad[1 : block_count + 1].reshape(shard_len, 2 * width_cols)
    core = (
        core.at[:block_len]
        .add(rim_sums[:block_len])
        .at[shard_len - block_len :]
        .add(rim_sums[3 * block_len :])
    )
    core = core.reshape(block_count, block_len, 2, head_count, head_dim)
    def give_back(terms):
        terms = terms.reshape(request_count, block_len * head_dim).astype(jnp.bfloat16)
        outgoing = jnp.dot(pick_hot.T, terms, preferred_element_type=jnp.float32).astype(
            jnp.bfloat16
        )
        outgoing = outgoing.reshape(seq_count, capacity, block_len, head_dim)
        incoming = lax.all_to_all(outgoing, "seq", split_axis=0, concat_axis=0, tiled=True)
        return jnp.dot(
            serve_hot.T, incoming.reshape(slot_total, -1), preferred_element_type=jnp.float32
        ).reshape(block_count, head_count, block_len, head_dim)

    added_vals = give_back(value_far)
    added_keys = give_back(key_far)
    added = jnp.stack([added_keys, added_vals], axis=3)
    core = core + jnp.transpose(added, (0, 2, 3, 1, 4))
    grad_k = core[:, :, 0].reshape(shard_len, width_cols).astype(jnp.bfloat16)
    grad_v = core[:, :, 1].reshape(shard_len, width_cols).astype(jnp.bfloat16)
    grad_q_rows = grad_q.reshape(shard_len, width_cols)
    def to_owners(rows):
        count = rows.shape[0]
        rows = rows.reshape(count, group_count, piece_len, width_cols)
        pieces = [lax.dynamic_index_in_dim(rows, head_index, axis=1, keepdims=False)]
        for shift in range(1, group_count):
            pairs = [(i, (i + shift) % group_count) for i in range(group_count)]
            sent = lax.dynamic_index_in_dim(
                rows, (head_index + shift) % group_count, axis=1, keepdims=False
            )
            pieces.append(lax.ppermute(sent, "head", pairs))
        pieces = jnp.stack(pieces)
        order = (head_index - jnp.arange(group_count, dtype=jnp.int32)) % group_count
        pieces = jnp.take(pieces, order, axis=0)
        return jnp.transpose(pieces, (1, 2, 0, 3)).reshape(
            count, 1, piece_len, group_count * width_cols
        )

    grad_queries = to_owners(grad_q_rows[None])[0]
    back = to_owners(jnp.stack([grad_k, grad_v]))
    grad_keys, grad_values = back[0], back[1]
    return (layer_out, grad_queries, grad_keys, grad_values, weight_grad)


def solution(mesh):
    in_specs = (
        P("dp", ("seq", "head"), None),
        P("dp", ("seq", "head"), None),
        P("dp", ("seq", "head"), None),
        P("seq", "head", None),
        P("head", None),
        P("dp", ("seq", "head"), None),
    )
    out_specs = (
        P("dp", ("seq", "head"), None),
        P("dp", ("seq", "head"), None),
        P("dp", ("seq", "head"), None),
        P("dp", ("seq", "head"), None),
        P("head", None),
    )
    return jax.shard_map(
        per_device, mesh=mesh, in_specs=in_specs, out_specs=out_specs, check_vma=False
    )
```

```python
import math

import jax
import jax.numpy as jnp
from jax import lax
from jax.sharding import PartitionSpec as P

HEAD_SIZE = 128
BLOCK_TOKENS = 64


def with_halo(block, sides, width):
    for axis, dim in sides:
        count = lax.axis_size(axis)
        forward = [(i, i + 1) for i in range(count - 1)]
        backward = [(target, source) for source, target in forward]
        low = lax.ppermute(
            lax.slice_in_dim(block, block.shape[dim] - width, None, axis=dim), axis, forward
        )
        high = lax.ppermute(lax.slice_in_dim(block, 0, width, axis=dim), axis, backward)
        block = jnp.concatenate([low, block, high], axis=dim)
    return block


def broadcast_first(block, axis, radix=4):
    count = lax.axis_size(axis)
    index = lax.axis_index(axis)
    stride = 1
    while stride * radix < count:
        stride *= radix
    while stride >= 1:
        span = stride * radix
        updated = block
        for m in range(1, radix):
            pairs = [(j, j + m * stride) for j in range(0, count, span) if j + m * stride < count]
            if pairs:
                got = lax.ppermute(block, axis, pairs)
                updated = jnp.where(index % span == m * stride, got, updated)
        block = updated
        stride //= radix
    return block


def reduce_to_first(block, axis, radix=4):
    count = lax.axis_size(axis)
    stride = 1
    while stride < count:
        span = stride * radix
        total = block
        for m in range(1, radix):
            pairs = [(j + m * stride, j) for j in range(0, count, span) if j + m * stride < count]
            if pairs:
                sent = lax.ppermute(block.astype(jnp.bfloat16), axis, pairs)
                total = total + sent.astype(block.dtype)
        block = total
        stride *= radix
    return block


def request_slots(rand_blocks, block_count, head_count, seq_count, capacity):
    requests = jnp.transpose(rand_blocks, (0, 2, 1)).reshape(-1)
    head_of = jnp.arange(requests.shape[0], dtype=jnp.int32) % head_count
    owners = requests // block_count
    offsets = requests % block_count
    one_hot = (owners[:, None] == jnp.arange(seq_count, dtype=jnp.int32)[None, :]).astype(
        jnp.bfloat16
    )
    count = requests.shape[0]
    lower = (
        jnp.arange(count, dtype=jnp.int32)[:, None] >= jnp.arange(count, dtype=jnp.int32)[None, :]
    ).astype(jnp.bfloat16)
    running = jnp.dot(lower, one_hot, preferred_element_type=jnp.float32)
    position = jnp.sum(one_hot.astype(jnp.float32) * (running - 1.0), axis=1).astype(jnp.int32)
    return owners, position, offsets * head_count + head_of


def gather_all(block, axis, radix=4):
    count = lax.axis_size(axis)
    if count != radix * radix:
        return lax.all_gather(block, axis, axis=0, tiled=False)
    index = lax.axis_index(axis)
    for stride in (1, radix):
        place = (index // stride) % radix
        pieces = [block]
        for m in range(1, radix):
            pairs = [
                (i, i - ((i // stride) % radix) * stride + (((i // stride) % radix + m) % radix) * stride)
                for i in range(count)
            ]
            pieces.append(lax.ppermute(block, axis, pairs))
        pieces = jnp.stack(pieces)
        order = (place - jnp.arange(radix, dtype=jnp.int32)) % radix
        block = jnp.take(pieces, order, axis=0)
        if stride > 1:
            block = block.reshape((radix * radix,) + block.shape[2:])
    return block


def per_device(queries, key_rows, values, rand_blocks, out_weight, cotangent):
    block_len = BLOCK_TOKENS
    head_dim = HEAD_SIZE
    seq_count = lax.axis_size("seq")
    seq_index = lax.axis_index("seq")
    group_count = lax.axis_size("head")
    piece_len = queries.shape[1]
    width_cols = queries.shape[2] // group_count
    stacked = jnp.concatenate([queries, key_rows, values], axis=0)
    stacked = jnp.transpose(stacked.reshape(3, piece_len, group_count, width_cols), (2, 0, 1, 3))
    stacked = lax.all_to_all(stacked, "head", split_axis=0, concat_axis=0, tiled=True)
    stacked = jnp.transpose(stacked, (1, 0, 2, 3)).reshape(3, group_count * piece_len, width_cols)
    q_rows = stacked[0]
    shard_len = q_rows.shape[0]
    head_count = width_cols // head_dim
    block_count = shard_len // block_len
    rand_count = rand_blocks.shape[2]
    key_value = jnp.concatenate([stacked[1], stacked[2]], axis=1)
    padded = with_halo(key_value, (("seq", 0),), block_len)
    first_block = broadcast_first(key_value[:block_len], "seq")
    request_count = rand_blocks.shape[0] * rand_blocks.shape[1] * rand_blocks.shape[2]
    capacity = 3 * request_count // (2 * seq_count)
    owners, position, codes = request_slots(
        rand_blocks, block_count, head_count, seq_count, capacity
    )
    slot_of = owners * capacity + position
    every_block = gather_all(rand_blocks, "seq")
    all_owners, all_position, all_codes = jax.vmap(
        lambda r: request_slots(r, block_count, head_count, seq_count, capacity)
    )(every_block)
    match = (all_owners[:, :, None] == seq_index) & (
        all_position[:, :, None] == jnp.arange(capacity, dtype=jnp.int32)[None, None, :]
    )
    asked_here = jnp.sum(jnp.where(match, all_codes[:, :, None] + 1, 0), axis=1) - 1
    slot_total = seq_count * capacity
    pair_count = block_count * head_count
    asked_flat = asked_here.reshape(slot_total)
    serve_hot = (
        asked_flat[:, None] == jnp.arange(pair_count, dtype=jnp.int32)[None, :]
    ).astype(jnp.bfloat16)
    pick_hot = (
        slot_of[:, None] == jnp.arange(slot_total, dtype=jnp.int32)[None, :]
    ).astype(jnp.bfloat16)
    kv_pairs = jnp.transpose(
        key_value.reshape(block_count, block_len, 2, head_count, head_dim), (2, 0, 3, 1, 4)
    ).reshape(2, pair_count, block_len * head_dim)

    def fetch(pairs):
        served = jnp.dot(serve_hot, pairs, preferred_element_type=jnp.float32).astype(jnp.bfloat16)
        served = served.reshape(seq_count, capacity, block_len, head_dim)
        received = lax.all_to_all(served, "seq", split_axis=0, concat_axis=0, tiled=True)
        picked = jnp.dot(
            pick_hot, received.reshape(slot_total, -1), preferred_element_type=jnp.float32
        ).astype(jnp.bfloat16)
        return picked.reshape(block_count, rand_count, head_count, block_len, head_dim)

    far_keys = fetch(kv_pairs[0])
    far_vals = fetch(kv_pairs[1])
    pair_view = padded.reshape(block_count + 2, block_len, 2, head_count, head_dim)
    window_pairs = jnp.stack(
        [pair_view[:block_count], pair_view[1 : block_count + 1], pair_view[2:]], axis=1
    ).reshape(block_count, 3 * block_len, 2, head_count, head_dim)
    window_keys = window_pairs[:, :, 0]
    window_vals = window_pairs[:, :, 1]
    first_pairs = first_block.reshape(block_len, 2, head_count, head_dim)
    first_keys = first_pairs[:, 0]
    first_vals = first_pairs[:, 1]
    global_ids = seq_index * block_count + jnp.arange(block_count, dtype=jnp.int32)
    block_total = seq_count * block_count
    window_live = jnp.stack([global_ids > 0, global_ids >= 0, global_ids < block_total - 1], axis=1)
    window_mask = jnp.repeat(window_live, block_len, axis=1)[None, :, None, :]
    query_blocks = q_rows.reshape(block_count, block_len, head_count, head_dim)
    softmax_scale = 1.0 / math.sqrt(head_dim)
    score_window = (
        jnp.einsum("ibhd,ikhd->hibk", query_blocks, window_keys, preferred_element_type=jnp.float32)
        * softmax_scale
    )
    score_first = (
        jnp.einsum("ibhd,khd->hibk", query_blocks, first_keys, preferred_element_type=jnp.float32)
        * softmax_scale
    )
    score_far = (
        jnp.einsum("ibhd,irhtd->hibrt", query_blocks, far_keys, preferred_element_type=jnp.float32)
        * softmax_scale
    )
    max_window = jnp.max(jnp.where(window_mask, score_window, -jnp.inf), axis=-1, keepdims=True)
    max_first = jnp.max(score_first, axis=-1, keepdims=True)
    max_far = jnp.max(score_far, axis=(-2, -1))[..., None]
    row_max = jnp.maximum(jnp.maximum(max_window, max_first), max_far)
    weight_window = jnp.where(window_mask, jnp.exp(score_window - row_max), 0.0)
    weight_first = jnp.exp(score_first - row_max)
    weight_far = jnp.exp(score_far - row_max[..., None])
    totals = (
        jnp.sum(weight_window, axis=-1, keepdims=True)
        + jnp.sum(weight_first, axis=-1, keepdims=True)
        + jnp.sum(weight_far, axis=(-2, -1))[..., None]
    )
    mixed = jnp.einsum(
        "hibk,ikhd->ibhd",
        weight_window.astype(jnp.bfloat16),
        window_vals,
        preferred_element_type=jnp.float32,
    )
    mixed = mixed + jnp.einsum(
        "hibk,khd->ibhd",
        weight_first.astype(jnp.bfloat16),
        first_vals,
        preferred_element_type=jnp.float32,
    )
    mixed = mixed + jnp.einsum(
        "hibrt,irhtd->ibhd",
        weight_far.astype(jnp.bfloat16),
        far_vals,
        preferred_element_type=jnp.float32,
    )
    totals_rows = jnp.transpose(totals, (1, 2, 0, 3))
    attn = (mixed / totals_rows).astype(jnp.bfloat16)
    logsum = row_max + jnp.log(totals)
    attn_rows = attn.reshape(shard_len, width_cols)
    layer_out = lax.psum_scatter(
        jnp.dot(attn_rows, out_weight, preferred_element_type=jnp.float32).astype(jnp.bfloat16),
        "head",
        scatter_dimension=0,
        tiled=True,
    )[None]
    piece_flat = lax.all_gather(cotangent, "head", axis=1, tiled=True)[0]
    grad_piece = jnp.dot(piece_flat, out_weight.T, preferred_element_type=jnp.float32).astype(
        jnp.bfloat16
    )
    weight_acc = jnp.dot(attn_rows.T, piece_flat, preferred_element_type=jnp.float32)
    token_total = lax.axis_size("dp") * seq_count * shard_len
    dp_index = lax.axis_index("dp")
    half_rows = width_cols // 2
    mine = lax.dynamic_slice_in_dim(weight_acc, dp_index * half_rows, half_rows, axis=0)
    theirs = lax.dynamic_slice_in_dim(weight_acc, (1 - dp_index) * half_rows, half_rows, axis=0)
    mine = mine + lax.ppermute(theirs, "dp", [(0, 1), (1, 0)])
    mine = lax.psum(mine.astype(jnp.bfloat16), "seq")
    other = lax.ppermute(mine, "dp", [(0, 1), (1, 0)])
    low = jnp.where(dp_index == 0, mine, other)
    high = jnp.where(dp_index == 0, other, mine)
    weight_grad = jnp.concatenate([low, high], axis=0).astype(jnp.float32) * (
        1.0 / math.sqrt(token_total)
    )
    grad_blocks = grad_piece.reshape(block_count, block_len, head_count, head_dim)
    delta_rows = jnp.sum(grad_blocks.astype(jnp.float32) * attn.astype(jnp.float32), axis=-1)
    row_delta = jnp.transpose(delta_rows, (2, 0, 1))[..., None]
    prob_window = jnp.where(window_mask, jnp.exp(score_window - logsum), 0.0)
    prob_first = jnp.exp(score_first - logsum)
    prob_far = jnp.exp(score_far - logsum[..., None])
    dprob_window = jnp.einsum(
        "ibhd,ikhd->hibk", grad_blocks, window_vals, preferred_element_type=jnp.float32
    )
    dprob_first = jnp.einsum(
        "ibhd,khd->hibk", grad_blocks, first_vals, preferred_element_type=jnp.float32
    )
    dprob_far = jnp.einsum(
        "ibhd,irhtd->hibrt", grad_blocks, far_vals, preferred_element_type=jnp.float32
    )
    dscore_window = (prob_window * (dprob_window - row_delta)).astype(jnp.bfloat16)
    dscore_first = (prob_first * (dprob_first - row_delta)).astype(jnp.bfloat16)
    dscore_far = (prob_far * (dprob_far - row_delta[..., None])).astype(jnp.bfloat16)
    grad_q = jnp.einsum(
        "hibk,ikhd->ibhd", dscore_window, window_keys, preferred_element_type=jnp.float32
    )
    grad_q = grad_q + jnp.einsum(
        "hibk,khd->ibhd", dscore_first, first_keys, preferred_element_type=jnp.float32
    )
    grad_q = grad_q + jnp.einsum(
        "hibrt,irhtd->ibhd", dscore_far, far_keys, preferred_element_type=jnp.float32
    )
    grad_q = (grad_q * softmax_scale).astype(jnp.bfloat16)
    key_window = (
        jnp.einsum(
            "hibk,ibhd->ikhd", dscore_window, query_blocks, preferred_element_type=jnp.float32
        )
        * softmax_scale
    )
    value_window = jnp.einsum(
        "hibk,ibhd->ikhd",
        prob_window.astype(jnp.bfloat16),
        grad_blocks,
        preferred_element_type=jnp.float32,
    )
    key_first = (
        jnp.einsum("hibk,ibhd->khd", dscore_first, query_blocks, preferred_element_type=jnp.float32)
        * softmax_scale
    )
    value_first = jnp.einsum(
        "hibk,ibhd->khd",
        prob_first.astype(jnp.bfloat16),
        grad_blocks,
        preferred_element_type=jnp.float32,
    )
    key_far = (
        jnp.einsum(
            "hibrt,ibhd->irhtd", dscore_far, query_blocks, preferred_element_type=jnp.float32
        )
        * softmax_scale
    )
    value_far = jnp.einsum(
        "hibrt,ibhd->irhtd",
        prob_far.astype(jnp.bfloat16),
        grad_blocks,
        preferred_element_type=jnp.float32,
    )
    window_terms = jnp.stack(
        [
            key_window.reshape(block_count, 3, block_len, head_count, head_dim),
            value_window.reshape(block_count, 3, block_len, head_count, head_dim),
        ],
        axis=3,
    )
    grad_pad = jnp.zeros((block_count + 2, block_len, 2, head_count, head_dim), jnp.float32)
    grad_pad = (
        grad_pad.at[:block_count]
        .add(window_terms[:, 0])
        .at[1 : block_count + 1]
        .add(window_terms[:, 1])
        .at[2:]
        .add(window_terms[:, 2])
    )
    global_grad = reduce_to_first(
        jnp.stack([key_first, value_first], axis=1).reshape(block_len, 2 * width_cols), "seq"
    ).reshape(block_len, 2, head_count, head_dim)
    grad_pad = grad_pad.at[1].add(jnp.where(seq_index == 0, global_grad, 0.0))
    rims = jnp.concatenate([grad_pad[0], grad_pad[block_count + 1]], axis=0).reshape(
        2 * block_len, 2 * width_cols
    )
    rim_sums = with_halo(rims.astype(jnp.bfloat16), (("seq", 0),), block_len).astype(rims.dtype)
    core = grad_pad[1 : block_count + 1].reshape(shard_len, 2 * width_cols)
    core = (
        core.at[:block_len]
        .add(rim_sums[:block_len])
        .at[shard_len - block_len :]
        .add(rim_sums[3 * block_len :])
    )
    core = core.reshape(block_count, block_len, 2, head_count, head_dim)
    def give_back(terms):
        terms = terms.reshape(request_count, block_len * head_dim).astype(jnp.bfloat16)
        outgoing = jnp.dot(pick_hot.T, terms, preferred_element_type=jnp.float32).astype(
            jnp.bfloat16
        )
        outgoing = outgoing.reshape(seq_count, capacity, block_len, head_dim)
        incoming = lax.all_to_all(outgoing, "seq", split_axis=0, concat_axis=0, tiled=True)
        return jnp.dot(
            serve_hot.T, incoming.reshape(slot_total, -1), preferred_element_type=jnp.float32
        ).reshape(block_count, head_count, block_len, head_dim)

    added_vals = give_back(value_far)
    added_keys = give_back(key_far)
    added = jnp.stack([added_keys, added_vals], axis=3)
    core = core + jnp.transpose(added, (0, 2, 3, 1, 4))
    grad_k = core[:, :, 0].reshape(shard_len, width_cols).astype(jnp.bfloat16)
    grad_v = core[:, :, 1].reshape(shard_len, width_cols).astype(jnp.bfloat16)
    grad_q_rows = grad_q.reshape(shard_len, width_cols)
    head_index = lax.axis_index("head")

    def to_owners(rows):
        count = rows.shape[0]
        rows = rows.reshape(count, group_count, piece_len, width_cols)
        pieces = [lax.dynamic_index_in_dim(rows, head_index, axis=1, keepdims=False)]
        for shift in range(1, group_count):
            pairs = [(i, (i + shift) % group_count) for i in range(group_count)]
            sent = lax.dynamic_index_in_dim(
                rows, (head_index + shift) % group_count, axis=1, keepdims=False
            )
            pieces.append(lax.ppermute(sent, "head", pairs))
        pieces = jnp.stack(pieces)
        order = (head_index - jnp.arange(group_count, dtype=jnp.int32)) % group_count
        pieces = jnp.take(pieces, order, axis=0)
        return jnp.transpose(pieces, (1, 2, 0, 3)).reshape(
            count, 1, piece_len, group_count * width_cols
        )

    grad_queries = to_owners(grad_q_rows[None])[0]
    back = to_owners(jnp.stack([grad_k, grad_v]))
    grad_keys, grad_values = back[0], back[1]
    return (layer_out, grad_queries, grad_keys, grad_values, weight_grad)


def solution(mesh):
    in_specs = (
        P("dp", ("seq", "head"), None),
        P("dp", ("seq", "head"), None),
        P("dp", ("seq", "head"), None),
        P("seq", "head", None),
        P("head", None),
        P("dp", ("seq", "head"), None),
    )
    out_specs = (
        P("dp", ("seq", "head"), None),
        P("dp", ("seq", "head"), None),
        P("dp", ("seq", "head"), None),
        P("dp", ("seq", "head"), None),
        P("head", None),
    )
    return jax.shard_map(
        per_device, mesh=mesh, in_specs=in_specs, out_specs=out_specs, check_vma=False
    )
```

```python
import math

import jax
import jax.numpy as jnp
from jax import lax
from jax.sharding import PartitionSpec as P

HEAD_SIZE = 128
BLOCK_TOKENS = 64


def with_halo(block, sides, width):
    for axis, dim in sides:
        count = lax.axis_size(axis)
        forward = [(i, i + 1) for i in range(count - 1)]
        backward = [(target, source) for source, target in forward]
        low = lax.ppermute(
            lax.slice_in_dim(block, block.shape[dim] - width, None, axis=dim), axis, forward
        )
        high = lax.ppermute(lax.slice_in_dim(block, 0, width, axis=dim), axis, backward)
        block = jnp.concatenate([low, block, high], axis=dim)
    return block


def broadcast_first(block, axis, radix=4):
    count = lax.axis_size(axis)
    index = lax.axis_index(axis)
    stride = 1
    while stride * radix < count:
        stride *= radix
    while stride >= 1:
        span = stride * radix
        updated = block
        for m in range(1, radix):
            pairs = [(j, j + m * stride) for j in range(0, count, span) if j + m * stride < count]
            if pairs:
                got = lax.ppermute(block, axis, pairs)
                updated = jnp.where(index % span == m * stride, got, updated)
        block = updated
        stride //= radix
    return block


def reduce_to_first(block, axis, radix=4):
    count = lax.axis_size(axis)
    stride = 1
    while stride < count:
        span = stride * radix
        total = block
        for m in range(1, radix):
            pairs = [(j + m * stride, j) for j in range(0, count, span) if j + m * stride < count]
            if pairs:
                sent = lax.ppermute(block.astype(jnp.bfloat16), axis, pairs)
                total = total + sent.astype(block.dtype)
        block = total
        stride *= radix
    return block


def request_slots(rand_blocks, block_count, head_count, seq_count, capacity):
    requests = jnp.transpose(rand_blocks, (0, 2, 1)).reshape(-1)
    head_of = jnp.arange(requests.shape[0], dtype=jnp.int32) % head_count
    owners = requests // block_count
    offsets = requests % block_count
    one_hot = (owners[:, None] == jnp.arange(seq_count, dtype=jnp.int32)[None, :]).astype(
        jnp.bfloat16
    )
    count = requests.shape[0]
    lower = (
        jnp.arange(count, dtype=jnp.int32)[:, None] >= jnp.arange(count, dtype=jnp.int32)[None, :]
    ).astype(jnp.bfloat16)
    running = jnp.dot(lower, one_hot, preferred_element_type=jnp.float32)
    position = jnp.sum(one_hot.astype(jnp.float32) * (running - 1.0), axis=1).astype(jnp.int32)
    return owners, position, offsets * head_count + head_of


def gather_all(block, axis, radix=4):
    count = lax.axis_size(axis)
    if count != radix * radix:
        return lax.all_gather(block, axis, axis=0, tiled=False)
    index = lax.axis_index(axis)
    for stride in (1, radix):
        place = (index // stride) % radix
        pieces = [block]
        for m in range(1, radix):
            pairs = [
                (i, i - ((i // stride) % radix) * stride + (((i // stride) % radix + m) % radix) * stride)
                for i in range(count)
            ]
            pieces.append(lax.ppermute(block, axis, pairs))
        pieces = jnp.stack(pieces)
        order = (place - jnp.arange(radix, dtype=jnp.int32)) % radix
        block = jnp.take(pieces, order, axis=0)
        if stride > 1:
            block = block.reshape((radix * radix,) + block.shape[2:])
    return block


def per_device(queries, key_rows, values, rand_blocks, out_weight, cotangent):
    block_len = BLOCK_TOKENS
    head_dim = HEAD_SIZE
    seq_count = lax.axis_size("seq")
    seq_index = lax.axis_index("seq")
    group_count = lax.axis_size("head")
    piece_len = queries.shape[1]
    width_cols = queries.shape[2] // group_count
    stacked = jnp.concatenate([queries, key_rows, values], axis=0)
    stacked = jnp.transpose(stacked.reshape(3, piece_len, group_count, width_cols), (2, 0, 1, 3))
    stacked = lax.all_to_all(stacked, "head", split_axis=0, concat_axis=0, tiled=True)
    stacked = jnp.transpose(stacked, (1, 0, 2, 3)).reshape(3, group_count * piece_len, width_cols)
    q_rows = stacked[0]
    shard_len = q_rows.shape[0]
    head_count = width_cols // head_dim
    block_count = shard_len // block_len
    rand_count = rand_blocks.shape[2]
    key_value = jnp.concatenate([stacked[1], stacked[2]], axis=1)
    padded = with_halo(key_value, (("seq", 0),), block_len)
    first_block = broadcast_first(key_value[:block_len], "seq")
    request_count = rand_blocks.shape[0] * rand_blocks.shape[1] * rand_blocks.shape[2]
    capacity = 3 * request_count // (2 * seq_count)
    owners, position, codes = request_slots(
        rand_blocks, block_count, head_count, seq_count, capacity
    )
    slot_of = owners * capacity + position
    every_block = gather_all(rand_blocks, "seq")
    all_owners, all_position, all_codes = jax.vmap(
        lambda r: request_slots(r, block_count, head_count, seq_count, capacity)
    )(every_block)
    match = (all_owners[:, :, None] == seq_index) & (
        all_position[:, :, None] == jnp.arange(capacity, dtype=jnp.int32)[None, None, :]
    )
    asked_here = jnp.sum(jnp.where(match, all_codes[:, :, None] + 1, 0), axis=1) - 1
    slot_total = seq_count * capacity
    pair_count = block_count * head_count
    asked_flat = asked_here.reshape(slot_total)
    serve_hot = (
        asked_flat[:, None] == jnp.arange(pair_count, dtype=jnp.int32)[None, :]
    ).astype(jnp.bfloat16)
    pick_hot = (
        slot_of[:, None] == jnp.arange(slot_total, dtype=jnp.int32)[None, :]
    ).astype(jnp.bfloat16)
    kv_pairs = jnp.transpose(
        key_value.reshape(block_count, block_len, 2, head_count, head_dim), (2, 0, 3, 1, 4)
    ).reshape(2, pair_count, block_len * head_dim)

    def fetch(pairs):
        served = jnp.dot(serve_hot, pairs, preferred_element_type=jnp.float32).astype(jnp.bfloat16)
        served = served.reshape(seq_count, capacity, block_len, head_dim)
        received = lax.all_to_all(served, "seq", split_axis=0, concat_axis=0, tiled=True)
        picked = jnp.dot(
            pick_hot, received.reshape(slot_total, -1), preferred_element_type=jnp.float32
        ).astype(jnp.bfloat16)
        return picked.reshape(block_count, rand_count, head_count, block_len, head_dim)

    far_keys = fetch(kv_pairs[0])
    far_vals = fetch(kv_pairs[1])
    pair_view = padded.reshape(block_count + 2, block_len, 2, head_count, head_dim)
    window_pairs = jnp.stack(
        [pair_view[:block_count], pair_view[1 : block_count + 1], pair_view[2:]], axis=1
    ).reshape(block_count, 3 * block_len, 2, head_count, head_dim)
    window_keys = window_pairs[:, :, 0]
    window_vals = window_pairs[:, :, 1]
    first_pairs = first_block.reshape(block_len, 2, head_count, head_dim)
    first_keys = first_pairs[:, 0]
    first_vals = first_pairs[:, 1]
    global_ids = seq_index * block_count + jnp.arange(block_count, dtype=jnp.int32)
    block_total = seq_count * block_count
    window_live = jnp.stack([global_ids > 0, global_ids >= 0, global_ids < block_total - 1], axis=1)
    window_mask = jnp.repeat(window_live, block_len, axis=1)[None, :, None, :]
    query_blocks = q_rows.reshape(block_count, block_len, head_count, head_dim)
    softmax_scale = 1.0 / math.sqrt(head_dim)
    score_window = (
        jnp.einsum("ibhd,ikhd->hibk", query_blocks, window_keys, preferred_element_type=jnp.float32)
        * softmax_scale
    )
    score_first = (
        jnp.einsum("ibhd,khd->hibk", query_blocks, first_keys, preferred_element_type=jnp.float32)
        * softmax_scale
    )
    score_far = (
        jnp.einsum("ibhd,irhtd->hibrt", query_blocks, far_keys, preferred_element_type=jnp.float32)
        * softmax_scale
    )
    max_window = jnp.max(jnp.where(window_mask, score_window, -jnp.inf), axis=-1, keepdims=True)
    max_first = jnp.max(score_first, axis=-1, keepdims=True)
    max_far = jnp.max(score_far, axis=(-2, -1))[..., None]
    row_max = jnp.maximum(jnp.maximum(max_window, max_first), max_far)
    weight_window = jnp.where(window_mask, jnp.exp(score_window - row_max), 0.0)
    weight_first = jnp.exp(score_first - row_max)
    weight_far = jnp.exp(score_far - row_max[..., None])
    totals = (
        jnp.sum(weight_window, axis=-1, keepdims=True)
        + jnp.sum(weight_first, axis=-1, keepdims=True)
        + jnp.sum(weight_far, axis=(-2, -1))[..., None]
    )
    mixed = jnp.einsum(
        "hibk,ikhd->ibhd",
        weight_window.astype(jnp.bfloat16),
        window_vals,
        preferred_element_type=jnp.float32,
    )
    mixed = mixed + jnp.einsum(
        "hibk,khd->ibhd",
        weight_first.astype(jnp.bfloat16),
        first_vals,
        preferred_element_type=jnp.float32,
    )
    mixed = mixed + jnp.einsum(
        "hibrt,irhtd->ibhd",
        weight_far.astype(jnp.bfloat16),
        far_vals,
        preferred_element_type=jnp.float32,
    )
    totals_rows = jnp.transpose(totals, (1, 2, 0, 3))
    attn = (mixed / totals_rows).astype(jnp.bfloat16)
    logsum = row_max + jnp.log(totals)
    attn_rows = attn.reshape(shard_len, width_cols)
    layer_out = lax.psum_scatter(
        jnp.dot(attn_rows, out_weight, preferred_element_type=jnp.float32).astype(jnp.bfloat16),
        "head",
        scatter_dimension=0,
        tiled=True,
    )[None]
    piece_flat = lax.all_gather(cotangent, "head", axis=1, tiled=True)[0]
    grad_piece = jnp.dot(piece_flat, out_weight.T, preferred_element_type=jnp.float32).astype(
        jnp.bfloat16
    )
    weight_acc = jnp.dot(attn_rows.T, piece_flat, preferred_element_type=jnp.float32)
    token_total = lax.axis_size("dp") * seq_count * shard_len
    dp_index = lax.axis_index("dp")
    half_rows = width_cols // 2
    mine = lax.dynamic_slice_in_dim(weight_acc, dp_index * half_rows, half_rows, axis=0)
    theirs = lax.dynamic_slice_in_dim(weight_acc, (1 - dp_index) * half_rows, half_rows, axis=0)
    mine = mine + lax.ppermute(theirs, "dp", [(0, 1), (1, 0)])
    mine = lax.psum(mine.astype(jnp.bfloat16), "seq").astype(jnp.float32) * (
        1.0 / math.sqrt(token_total)
    )
    other = lax.ppermute(mine, "dp", [(0, 1), (1, 0)])
    weight_grad = jnp.where(
        dp_index == 0,
        jnp.concatenate([mine, other], axis=0),
        jnp.concatenate([other, mine], axis=0),
    )
    grad_blocks = grad_piece.reshape(block_count, block_len, head_count, head_dim)
    delta_rows = jnp.sum(grad_blocks.astype(jnp.float32) * attn.astype(jnp.float32), axis=-1)
    row_delta = jnp.transpose(delta_rows, (2, 0, 1))[..., None]
    prob_window = jnp.where(window_mask, jnp.exp(score_window - logsum), 0.0)
    prob_first = jnp.exp(score_first - logsum)
    prob_far = jnp.exp(score_far - logsum[..., None])
    dprob_window = jnp.einsum(
        "ibhd,ikhd->hibk", grad_blocks, window_vals, preferred_element_type=jnp.float32
    )
    dprob_first = jnp.einsum(
        "ibhd,khd->hibk", grad_blocks, first_vals, preferred_element_type=jnp.float32
    )
    dprob_far = jnp.einsum(
        "ibhd,irhtd->hibrt", grad_blocks, far_vals, preferred_element_type=jnp.float32
    )
    dscore_window = (prob_window * (dprob_window - row_delta)).astype(jnp.bfloat16)
    dscore_first = (prob_first * (dprob_first - row_delta)).astype(jnp.bfloat16)
    dscore_far = (prob_far * (dprob_far - row_delta[..., None])).astype(jnp.bfloat16)
    grad_q = jnp.einsum(
        "hibk,ikhd->ibhd", dscore_window, window_keys, preferred_element_type=jnp.float32
    )
    grad_q = grad_q + jnp.einsum(
        "hibk,khd->ibhd", dscore_first, first_keys, preferred_element_type=jnp.float32
    )
    grad_q = grad_q + jnp.einsum(
        "hibrt,irhtd->ibhd", dscore_far, far_keys, preferred_element_type=jnp.float32
    )
    grad_q = (grad_q * softmax_scale).astype(jnp.bfloat16)
    key_window = (
        jnp.einsum(
            "hibk,ibhd->ikhd", dscore_window, query_blocks, preferred_element_type=jnp.float32
        )
        * softmax_scale
    )
    value_window = jnp.einsum(
        "hibk,ibhd->ikhd",
        prob_window.astype(jnp.bfloat16),
        grad_blocks,
        preferred_element_type=jnp.float32,
    )
    key_first = (
        jnp.einsum("hibk,ibhd->khd", dscore_first, query_blocks, preferred_element_type=jnp.float32)
        * softmax_scale
    )
    value_first = jnp.einsum(
        "hibk,ibhd->khd",
        prob_first.astype(jnp.bfloat16),
        grad_blocks,
        preferred_element_type=jnp.float32,
    )
    key_far = (
        jnp.einsum(
            "hibrt,ibhd->irhtd", dscore_far, query_blocks, preferred_element_type=jnp.float32
        )
        * softmax_scale
    )
    value_far = jnp.einsum(
        "hibrt,ibhd->irhtd",
        prob_far.astype(jnp.bfloat16),
        grad_blocks,
        preferred_element_type=jnp.float32,
    )
    window_terms = jnp.stack(
        [
            key_window.reshape(block_count, 3, block_len, head_count, head_dim),
            value_window.reshape(block_count, 3, block_len, head_count, head_dim),
        ],
        axis=3,
    )
    grad_pad = jnp.zeros((block_count + 2, block_len, 2, head_count, head_dim), jnp.float32)
    grad_pad = (
        grad_pad.at[:block_count]
        .add(window_terms[:, 0])
        .at[1 : block_count + 1]
        .add(window_terms[:, 1])
        .at[2:]
        .add(window_terms[:, 2])
    )
    global_grad = reduce_to_first(
        jnp.stack([key_first, value_first], axis=1).reshape(block_len, 2 * width_cols), "seq"
    ).reshape(block_len, 2, head_count, head_dim)
    grad_pad = grad_pad.at[1].add(jnp.where(seq_index == 0, global_grad, 0.0))
    rims = jnp.concatenate([grad_pad[0], grad_pad[block_count + 1]], axis=0).reshape(
        2 * block_len, 2 * width_cols
    )
    rim_sums = with_halo(rims.astype(jnp.bfloat16), (("seq", 0),), block_len).astype(rims.dtype)
    core = grad_pad[1 : block_count + 1].reshape(shard_len, 2 * width_cols)
    core = (
        core.at[:block_len]
        .add(rim_sums[:block_len])
        .at[shard_len - block_len :]
        .add(rim_sums[3 * block_len :])
    )
    core = core.reshape(block_count, block_len, 2, head_count, head_dim)
    def give_back(terms):
        terms = terms.reshape(request_count, block_len * head_dim).astype(jnp.bfloat16)
        outgoing = jnp.dot(pick_hot.T, terms, preferred_element_type=jnp.float32).astype(
            jnp.bfloat16
        )
        outgoing = outgoing.reshape(seq_count, capacity, block_len, head_dim)
        incoming = lax.all_to_all(outgoing, "seq", split_axis=0, concat_axis=0, tiled=True)
        return jnp.dot(
            serve_hot.T, incoming.reshape(slot_total, -1), preferred_element_type=jnp.float32
        ).reshape(block_count, head_count, block_len, head_dim)

    added_vals = give_back(value_far)
    added_keys = give_back(key_far)
    added = jnp.stack([added_keys, added_vals], axis=3)
    core = core + jnp.transpose(added, (0, 2, 3, 1, 4))
    grad_k = core[:, :, 0].reshape(shard_len, width_cols).astype(jnp.bfloat16)
    grad_v = core[:, :, 1].reshape(shard_len, width_cols).astype(jnp.bfloat16)
    grad_q_rows = grad_q.reshape(shard_len, width_cols)
    head_index = lax.axis_index("head")

    def to_owners(rows):
        count = rows.shape[0]
        rows = rows.reshape(count, group_count, piece_len, width_cols)
        pieces = [lax.dynamic_index_in_dim(rows, head_index, axis=1, keepdims=False)]
        for shift in range(1, group_count):
            pairs = [(i, (i + shift) % group_count) for i in range(group_count)]
            sent = lax.dynamic_index_in_dim(
                rows, (head_index + shift) % group_count, axis=1, keepdims=False
            )
            pieces.append(lax.ppermute(sent, "head", pairs))
        pieces = jnp.stack(pieces)
        order = (head_index - jnp.arange(group_count, dtype=jnp.int32)) % group_count
        pieces = jnp.take(pieces, order, axis=0)
        return jnp.transpose(pieces, (1, 2, 0, 3)).reshape(
            count, 1, piece_len, group_count * width_cols
        )

    grad_queries = to_owners(grad_q_rows[None])[0]
    back = to_owners(jnp.stack([grad_k, grad_v]))
    grad_keys, grad_values = back[0], back[1]
    return (layer_out, grad_queries, grad_keys, grad_values, weight_grad)


def solution(mesh):
    in_specs = (
        P("dp", ("seq", "head"), None),
        P("dp", ("seq", "head"), None),
        P("dp", ("seq", "head"), None),
        P("seq", "head", None),
        P("head", None),
        P("dp", ("seq", "head"), None),
    )
    out_specs = (
        P("dp", ("seq", "head"), None),
        P("dp", ("seq", "head"), None),
        P("dp", ("seq", "head"), None),
        P("dp", ("seq", "head"), None),
        P("head", None),
    )
    return jax.shard_map(
        per_device, mesh=mesh, in_specs=in_specs, out_specs=out_specs, check_vma=False
    )
```
